32 devices in a mesh: ev: 8 (over z, y), col: 4 (over x, core).
Axes of the slice: x: 2, y: 2, z: 4, core: 2. Of those that a mesh axis runs over, the one named last changes fastest.
Arguments:
- panel: bfloat16 [256, 131072], P('col', 'ev'), may hold values from -12 to 12
- signs: int32 [131072], P('ev'), may hold values from -1 to 1, as said below
- offsets: int32 [2048], replicated, may hold values from 0 to 63
Outputs:
- gram: float32 [256, 256], P('col')
The draws below stay inside these ranges and needn't reach their ends.
Inputs may be any that keep to these rules, and one draw needn't show every extreme that they name: `signs`: every entry is -1 or +1.
All inputs are finite; a program needn't handle non-finite values.
Results may differ from the reference program's by a relative error of at most 0.0003.
Values sent between devices are 32-bit elements; how exact they have to be, the bound alone decides.
No kernel may reach another device: no remote copies, remote signals or barrier semaphores. Data moves between devices by JAX's collectives and lax.ppermute only.
A program may use at most 64 MiB of HBM per device.

```python
import math
import jax
import jax.numpy as jnp
from jax import lax

C = 256
STRIDE = 64
EV_DEV = 16384
EVENTS = 131072
SAMPLES = 2048
N_EV = 8


def draw_panel(key, part):
    key_main, key_cols = jax.random.split(key, 2)
    col_scale = jnp.exp(jax.random.uniform(key_cols, (C, 1), jnp.float32, math.log(0.3), math.log(3.0)))
    values = jax.random.normal(key_main, (C, EVENTS), jnp.float32) * col_scale
    return jnp.clip(values, -12.0, 12.0).astype(jnp.bfloat16)


def draw_signs(key, part):
    return (2 * jax.random.randint(key, (EVENTS,), 0, 2) - 1).astype(jnp.int32)


def touch_ends(entries, stream_key, least, high):
    index_at = [jax.random.randint(jax.random.fold_in(stream_key, axis), (), 0, length) for axis, length in enumerate(entries.shape)]
    longest = entries.shape.index(max(entries.shape))
    neighbour = index_at[:longest] + [(index_at[longest] + 1) % entries.shape[longest]] + index_at[longest + 1:]
    return entries.at[tuple(index_at)].set(least).at[tuple(neighbour)].set(high)


def setup_inputs(seed: int = 0) -> dict:
    key_of = jax.random.split(jax.random.key(seed), 4)
    return {
        "panel": draw_panel(jax.random.fold_in(key_of[3], 71), 0),
        "signs": draw_signs(jax.random.fold_in(key_of[3], 71), 0),
        "offsets": touch_ends(jax.random.randint(key_of[2], (SAMPLES,), 0, STRIDE), jax.random.fold_in(key_of[2], 1), 0, STRIDE - 1).astype(jnp.int32),
    }


def hadamard(order):
    index = jnp.arange(order, dtype=jnp.int32)
    both = index[:, None] & index[None, :]
    parity = jnp.zeros((order, order), jnp.int32)
    for level in range(order.bit_length() - 1):
        parity = parity + (both >> level & 1)
    return (1 - 2 * (parity % 2)).astype(jnp.float32)

def reference(panel, signs, offsets):
    inner_len = EV_DEV // 128
    values = panel.astype(jnp.float32) * signs.astype(jnp.float32)[None, :]
    values = values.reshape(C, N_EV, 128, inner_len)
    high = lax.Precision.HIGHEST
    values = jnp.einsum('pq,cqab->cpab', hadamard(N_EV), values, precision=high)
    values = jnp.einsum('xa,cpab->cpxb', hadamard(128), values, precision=high)
    values = jnp.einsum('yb,cpxb->cpxy', hadamard(inner_len), values, precision=high)
    strata = values.reshape(C, SAMPLES, STRIDE)
    picked = jnp.take_along_axis(strata, offsets.astype(jnp.int32)[None, :, None], axis=2)[:, :, 0]
    sketch = picked * (1.0 / math.sqrt(SAMPLES * EVENTS))
    return jnp.dot(sketch, sketch.T, precision=high, preferred_element_type=jnp.float32)
```

```python
import math

import jax
import jax.numpy as jnp
from jax import lax
from jax.sharding import PartitionSpec as P

STRIDE = 64
OUTER = 128


def hadamard(order):
    index = jnp.arange(order, dtype=jnp.int32)
    both = index[:, None] & index[None, :]
    parity = jnp.zeros((order, order), jnp.int32)
    for level in range(order.bit_length() - 1):
        parity = parity + (both >> level & 1)
    return (1 - 2 * (parity % 2)).astype(jnp.float32)


def exchange(value, axis, bit):
    mask = 1 << bit
    pairs = [(source, source ^ mask) for source in range(lax.axis_size(axis))]
    return lax.ppermute(value, axis, pairs)


def split3(value):
    hi = lax.reduce_precision(value, exponent_bits=8, mantissa_bits=7)
    rest = value - hi
    mid = lax.reduce_precision(rest, exponent_bits=8, mantissa_bits=7)
    low = rest - mid
    return tuple(piece.astype(jnp.bfloat16) for piece in (hi, mid, low))


def selection(offsets, my_index, groups, inner):
    per_row = inner // STRIDE
    off = offsets.reshape(groups, OUTER, per_row)
    rows = jnp.arange(per_row, dtype=jnp.int32)[None, None, :] * STRIDE + off
    rows = rows.transpose(1, 0, 2)
    lanes = jnp.arange(inner, dtype=jnp.int32)
    parity = lax.population_count(rows[:, None, :, :] & lanes[None, :, None, None]) & 1
    group_parity = lax.population_count(jnp.arange(groups, dtype=jnp.int32) & my_index) & 1
    parity = parity ^ group_parity[None, None, :, None]
    return (1 - 2 * parity).astype(jnp.bfloat16).reshape(OUTER, inner, groups * per_row)


def per_device(panel, signs, offsets):
    columns, length = panel.shape
    groups = lax.axis_size("ev")
    levels = groups.bit_length() - 1
    my_index = lax.axis_index("ev")
    inner = length // OUTER
    per_row = inner // STRIDE
    high = lax.Precision.HIGHEST

    signed = panel * signs.astype(jnp.bfloat16)[None, :]
    blocks = signed.reshape(columns, OUTER, inner)
    first = jnp.einsum(
        "xa,cab->xcb",
        hadamard(OUTER).astype(jnp.bfloat16),
        blocks,
        preferred_element_type=jnp.float32,
    )
    pick = selection(offsets, my_index, groups, inner)
    pieces = jnp.concatenate(split3(first), axis=1)
    sampled = jnp.einsum("xcb,xbj->xcj", pieces, pick, preferred_element_type=jnp.float32)
    sampled = sampled[:, :columns] + sampled[:, columns : 2 * columns] + sampled[:, 2 * columns :]
    chunks = sampled.reshape(OUTER, columns, groups, per_row).transpose(2, 1, 0, 3)
    chunks = chunks.reshape([2] * levels + [columns, OUTER * per_row])
    chunks = chunks.transpose(list(range(levels))[::-1] + [levels, levels + 1])
    for level in range(levels):
        bit = my_index >> level & 1
        keep = lax.dynamic_index_in_dim(chunks, bit, axis=0, keepdims=False)
        send = lax.dynamic_index_in_dim(chunks, 1 - bit, axis=0, keepdims=False)
        chunks = keep + exchange(send, "ev", level)

    total_events = length * groups
    scale = 1.0 / math.sqrt(total_events * (total_events // STRIDE))
    sketch = chunks * scale
    partial_gram = jnp.dot(
        sketch,
        lax.all_gather(sketch, "col", axis=0, tiled=True).T,
        precision=high,
        preferred_element_type=jnp.float32,
    )
    for level in range(levels):
        partial_gram = partial_gram + exchange(partial_gram, "ev", level)
    return partial_gram


def solution(mesh):
    return jax.shard_map(
        per_device,
        mesh=mesh,
        in_specs=(P("col", "ev"), P("ev"), P()),
        out_specs=P("col", None),
        check_vma=False,
    )
```

```python
import math

import jax
import jax.numpy as jnp
from jax import lax
from jax.sharding import PartitionSpec as P

STRIDE = 64
OUTER = 128


def hadamard(order):
    index = jnp.arange(order, dtype=jnp.int32)
    both = index[:, None] & index[None, :]
    parity = jnp.zeros((order, order), jnp.int32)
    for level in range(order.bit_length() - 1):
        parity = parity + (both >> level & 1)
    return (1 - 2 * (parity % 2)).astype(jnp.float32)


def exchange(value, axis, bit):
    mask = 1 << bit
    pairs = [(source, source ^ mask) for source in range(lax.axis_size(axis))]
    return lax.ppermute(value, axis, pairs)


def split3(value):
    hi = lax.reduce_precision(value, exponent_bits=8, mantissa_bits=7)
    rest = value - hi
    mid = lax.reduce_precision(rest, exponent_bits=8, mantissa_bits=7)
    low = rest - mid
    return tuple(piece.astype(jnp.bfloat16) for piece in (hi, mid, low))


def selection(offsets, my_index, groups, inner):
    per_row = inner // STRIDE
    off = offsets.reshape(groups, OUTER, per_row)
    rows = jnp.arange(per_row, dtype=jnp.int32)[None, None, :] * STRIDE + off
    rows = rows.transpose(1, 0, 2)
    lanes = jnp.arange(inner, dtype=jnp.int32)
    parity = lax.population_count(rows[:, None, :, :] & lanes[None, :, None, None]) & 1
    group_parity = lax.population_count(jnp.arange(groups, dtype=jnp.int32) & my_index) & 1
    parity = parity ^ group_parity[None, None, :, None]
    return (1 - 2 * parity).astype(jnp.bfloat16).reshape(OUTER, inner, groups * per_row)


def per_device(panel, signs, offsets):
    columns, length = panel.shape
    groups = lax.axis_size("ev")
    levels = groups.bit_length() - 1
    my_index = lax.axis_index("ev")
    inner = length // OUTER
    per_row = inner // STRIDE
    high = lax.Precision.HIGHEST

    signed = panel * signs.astype(jnp.bfloat16)[None, :]
    blocks = signed.reshape(columns, OUTER, inner)
    first = jnp.einsum(
        "xa,cab->xcb",
        hadamard(OUTER).astype(jnp.bfloat16),
        blocks,
        preferred_element_type=jnp.float32,
    )
    pick = selection(offsets, my_index, groups, inner)
    pieces = jnp.concatenate(split3(first), axis=1)
    sampled = jnp.einsum("xcb,xbj->xcj", pieces, pick, preferred_element_type=jnp.float32)
    sampled = sampled[:, :columns] + sampled[:, columns : 2 * columns] + sampled[:, 2 * columns :]
    chunks = sampled.reshape(OUTER, columns, groups, per_row).transpose(2, 1, 0, 3)
    chunks = chunks.reshape(groups, columns, OUTER * per_row)
    chunks = lax.all_to_all(chunks, "ev", 0, 0, tiled=True).sum(axis=0)

    total_events = length * groups
    scale = 1.0 / math.sqrt(total_events * (total_events // STRIDE))
    sketch = chunks * scale
    partial_gram = jnp.dot(
        sketch,
        lax.all_gather(sketch, "col", axis=0, tiled=True).T,
        precision=high,
        preferred_element_type=jnp.float32,
    )
    return lax.all_gather(partial_gram, "ev").sum(axis=0)


def solution(mesh):
    return jax.shard_map(
        per_device,
        mesh=mesh,
        in_specs=(P("col", "ev"), P("ev"), P()),
        out_specs=P("col", None),
        check_vma=False,
    )
```

```python
import math

import jax
import jax.numpy as jnp
from jax import lax
from jax.sharding import PartitionSpec as P

STRIDE = 64
OUTER = 128


def hadamard(order):
    index = jnp.arange(order, dtype=jnp.int32)
    both = index[:, None] & index[None, :]
    parity = jnp.zeros((order, order), jnp.int32)
    for level in range(order.bit_length() - 1):
        parity = parity + (both >> level & 1)
    return (1 - 2 * (parity % 2)).astype(jnp.float32)


def exchange(value, axis, bit):
    mask = 1 << bit
    pairs = [(source, source ^ mask) for source in range(lax.axis_size(axis))]
    return lax.ppermute(value, axis, pairs)


def split3(value):
    hi = lax.reduce_precision(value, exponent_bits=8, mantissa_bits=7)
    rest = value - hi
    mid = lax.reduce_precision(rest, exponent_bits=8, mantissa_bits=7)
    low = rest - mid
    return tuple(piece.astype(jnp.bfloat16) for piece in (hi, mid, low))


def selection(offsets, my_index, groups, inner):
    per_row = inner // STRIDE
    off = offsets.reshape(groups, OUTER, per_row)
    rows = jnp.arange(per_row, dtype=jnp.int32)[None, None, :] * STRIDE + off
    rows = rows.transpose(1, 0, 2)
    lanes = jnp.arange(inner, dtype=jnp.int32)
    parity = lax.population_count(rows[:, None, :, :] & lanes[None, :, None, None]) & 1
    group_parity = lax.population_count(jnp.arange(groups, dtype=jnp.int32) & my_index) & 1
    parity = parity ^ group_parity[None, None, :, None]
    return (1 - 2 * parity).astype(jnp.bfloat16).reshape(OUTER, inner, groups * per_row)


def per_device(panel, signs, offsets):
    columns, length = panel.shape
    groups = lax.axis_size("ev")
    levels = groups.bit_length() - 1
    my_index = lax.axis_index("ev")
    inner = length // OUTER
    per_row = inner // STRIDE
    high = lax.Precision.HIGHEST

    signed = panel * signs.astype(jnp.bfloat16)[None, :]
    blocks = signed.reshape(columns, OUTER, inner)
    first = jnp.einsum(
        "xa,cab->xcb",
        hadamard(OUTER).astype(jnp.bfloat16),
        blocks,
        preferred_element_type=jnp.float32,
    )
    pick = selection(offsets, my_index, groups, inner)
    pieces = jnp.concatenate(split3(first), axis=1)
    sampled = jnp.einsum("xcb,xbj->xcj", pieces, pick, preferred_element_type=jnp.float32)
    sampled = sampled[:, :columns] + sampled[:, columns : 2 * columns] + sampled[:, 2 * columns :]
    chunks = sampled.reshape(OUTER, columns, groups, per_row).transpose(2, 1, 0, 3)
    chunks = chunks.reshape(groups, columns, OUTER * per_row)
    chunks = lax.all_to_all(chunks, "ev", 0, 0, tiled=True).sum(axis=0)

    total_events = length * groups
    scale = 1.0 / math.sqrt(total_events * (total_events // STRIDE))
    sketch = chunks * scale
    partial_gram = jnp.dot(
        sketch,
        lax.all_gather(sketch, "col", axis=0, tiled=True).T,
        precision=high,
        preferred_element_type=jnp.float32,
    )
    for level in range(levels):
        partial_gram = partial_gram + exchange(partial_gram, "ev", level)
    return partial_gram


def solution(mesh):
    return jax.shard_map(
        per_device,
        mesh=mesh,
        in_specs=(P("col", "ev"), P("ev"), P()),
        out_specs=P("col", None),
        check_vma=False,
    )
```

```python
import math

import jax
import jax.numpy as jnp
from jax import lax
from jax.sharding import PartitionSpec as P

STRIDE = 64
OUTER = 128


def hadamard(order):
    index = jnp.arange(order, dtype=jnp.int32)
    both = index[:, None] & index[None, :]
    parity = jnp.zeros((order, order), jnp.int32)
    for level in range(order.bit_length() - 1):
        parity = parity + (both >> level & 1)
    return (1 - 2 * (parity % 2)).astype(jnp.float32)


def exchange(value, axis, bit):
    mask = 1 << bit
    pairs = [(source, source ^ mask) for source in range(lax.axis_size(axis))]
    return lax.ppermute(value, axis, pairs)


def split3(value):
    hi = lax.reduce_precision(value, exponent_bits=8, mantissa_bits=7)
    rest = value - hi
    mid = lax.reduce_precision(rest, exponent_bits=8, mantissa_bits=7)
    low = rest - mid
    return tuple(piece.astype(jnp.bfloat16) for piece in (hi, mid, low))


def selection(offsets, my_index, groups, inner):
    per_row = inner // STRIDE
    off = offsets.reshape(groups, OUTER, per_row)
    rows = jnp.arange(per_row, dtype=jnp.int32)[None, None, :] * STRIDE + off
    rows = rows.transpose(1, 0, 2)
    lanes = jnp.arange(inner, dtype=jnp.int32)
    parity = lax.population_count(rows[:, None, :, :] & lanes[None, :, None, None]) & 1
    group_parity = lax.population_count(jnp.arange(groups, dtype=jnp.int32) & my_index) & 1
    parity = parity ^ group_parity[None, None, :, None]
    return (1 - 2 * parity).astype(jnp.bfloat16).reshape(OUTER, inner, groups * per_row)


def per_device(panel, signs, offsets):
    columns, length = panel.shape
    groups = lax.axis_size("ev")
    levels = groups.bit_length() - 1
    my_index = lax.axis_index("ev")
    inner = length // OUTER
    per_row = inner // STRIDE
    high = lax.Precision.HIGHEST

    signed = panel * signs.astype(jnp.bfloat16)[None, :]
    blocks = signed.reshape(columns, OUTER, inner)
    first = jnp.einsum(
        "xa,cab->xcb",
        hadamard(OUTER).astype(jnp.bfloat16),
        blocks,
        preferred_element_type=jnp.float32,
    )
    pick = selection(offsets, my_index, groups, inner)
    sampled = jnp.einsum(
        "xcb,xbj->xcj",
        first,
        pick.astype(jnp.float32),
        precision=lax.Precision.HIGH,
        preferred_element_type=jnp.float32,
    )
    chunks = sampled.reshape(OUTER, columns, groups, per_row).transpose(2, 1, 0, 3)
    chunks = chunks.reshape(groups, columns, OUTER * per_row)
    chunks = lax.all_to_all(chunks, "ev", 0, 0, tiled=True).sum(axis=0)

    total_events = length * groups
    scale = 1.0 / math.sqrt(total_events * (total_events // STRIDE))
    sketch = chunks * scale
    partial_gram = jnp.dot(
        sketch,
        lax.all_gather(sketch, "col", axis=0, tiled=True).T,
        precision=high,
        preferred_element_type=jnp.float32,
    )
    for level in range(levels):
        partial_gram = partial_gram + exchange(partial_gram, "ev", level)
    return partial_gram


def solution(mesh):
    return jax.shard_map(
        per_device,
        mesh=mesh,
        in_specs=(P("col", "ev"), P("ev"), P()),
        out_specs=P("col", None),
        check_vma=False,
    )
```

```python
import math

import jax
import jax.numpy as jnp
from jax import lax
from jax.sharding import PartitionSpec as P

STRIDE = 64
OUTER = 128


def hadamard(order):
    index = jnp.arange(order, dtype=jnp.int32)
    both = index[:, None] & index[None, :]
    parity = jnp.zeros((order, order), jnp.int32)
    for level in range(order.bit_length() - 1):
        parity = parity + (both >> level & 1)
    return (1 - 2 * (parity % 2)).astype(jnp.float32)


def exchange(value, axis, bit):
    mask = 1 << bit
    pairs = [(source, source ^ mask) for source in range(lax.axis_size(axis))]
    return lax.ppermute(value, axis, pairs)


def split3(value):
    hi = lax.reduce_precision(value, exponent_bits=8, mantissa_bits=7)
    rest = value - hi
    mid = lax.reduce_precision(rest, exponent_bits=8, mantissa_bits=7)
    low = rest - mid
    return tuple(piece.astype(jnp.bfloat16) for piece in (hi, mid, low))


def selection(offsets, my_index, groups, inner):
    per_row = inner // STRIDE
    off = offsets.reshape(groups, OUTER, per_row)
    rows = jnp.arange(per_row, dtype=jnp.int32)[None, None, :] * STRIDE + off
    rows = rows.transpose(1, 0, 2)
    lanes = jnp.arange(inner, dtype=jnp.int32)
    parity = lax.population_count(rows[:, None, :, :] & lanes[None, :, None, None]) & 1
    group_parity = lax.population_count(jnp.arange(groups, dtype=jnp.int32) & my_index) & 1
    parity = parity ^ group_parity[None, None, :, None]
    return (1 - 2 * parity).astype(jnp.bfloat16).reshape(OUTER, inner, groups * per_row)


def per_device(panel, signs, offsets):
    columns, length = panel.shape
    groups = lax.axis_size("ev")
    levels = groups.bit_length() - 1
    my_index = lax.axis_index("ev")
    inner = length // OUTER
    per_row = inner // STRIDE
    high = lax.Precision.HIGHEST

    signed = panel * signs.astype(jnp.bfloat16)[None, :]
    blocks = signed.reshape(columns, OUTER, inner)
    first = jnp.einsum(
        "xa,cab->xcb",
        hadamard(OUTER).astype(jnp.bfloat16),
        blocks,
        preferred_element_type=jnp.float32,
    )
    pick = selection(offsets, my_index, groups, inner)
    sampled = jnp.einsum(
        "xcb,xbj->xcj",
        first,
        pick.astype(jnp.float32),
        precision=lax.Precision.HIGH,
        preferred_element_type=jnp.float32,
    )
    chunks = sampled.reshape(OUTER, columns, groups, per_row).transpose(2, 1, 0, 3)
    chunks = chunks.reshape(groups, columns, OUTER * per_row)
    own = lax.dynamic_index_in_dim(chunks, my_index, axis=0, keepdims=False)
    arrived = []
    for distance in range(1, groups):
        target = my_index ^ distance
        block = lax.dynamic_index_in_dim(chunks, target, axis=0, keepdims=False)
        pairs = [(source, source ^ distance) for source in range(groups)]
        arrived.append(lax.ppermute(block, "ev", pairs))
    chunks = own
    for block in arrived:
        chunks = chunks + block

    total_events = length * groups
    scale = 1.0 / math.sqrt(total_events * (total_events // STRIDE))
    sketch = chunks * scale
    partial_gram = jnp.dot(
        sketch,
        lax.all_gather(sketch, "col", axis=0, tiled=True).T,
        precision=high,
        preferred_element_type=jnp.float32,
    )
    for level in range(levels):
        partial_gram = partial_gram + exchange(partial_gram, "ev", level)
    return partial_gram


def solution(mesh):
    return jax.shard_map(
        per_device,
        mesh=mesh,
        in_specs=(P("col", "ev"), P("ev"), P()),
        out_specs=P("col", None),
        check_vma=False,
    )
```

```python
import math

import jax
import jax.numpy as jnp
from jax import lax
from jax.sharding import PartitionSpec as P

STRIDE = 64
OUTER = 128


def hadamard(order):
    index = jnp.arange(order, dtype=jnp.int32)
    both = index[:, None] & index[None, :]
    parity = jnp.zeros((order, order), jnp.int32)
    for level in range(order.bit_length() - 1):
        parity = parity + (both >> level & 1)
    return (1 - 2 * (parity % 2)).astype(jnp.float32)


def exchange(value, axis, bit):
    mask = 1 << bit
    pairs = [(source, source ^ mask) for source in range(lax.axis_size(axis))]
    return lax.ppermute(value, axis, pairs)


def split3(value):
    hi = lax.reduce_precision(value, exponent_bits=8, mantissa_bits=7)
    rest = value - hi
    mid = lax.reduce_precision(rest, exponent_bits=8, mantissa_bits=7)
    low = rest - mid
    return tuple(piece.astype(jnp.bfloat16) for piece in (hi, mid, low))


def selection(offsets, my_index, groups, inner):
    per_row = inner // STRIDE
    off = offsets.reshape(groups, OUTER, per_row)
    rows = jnp.arange(per_row, dtype=jnp.int32)[None, None, :] * STRIDE + off
    rows = rows.transpose(1, 0, 2)
    lanes = jnp.arange(inner, dtype=jnp.int32)
    parity = lax.population_count(rows[:, None, :, :] & lanes[None, :, None, None]) & 1
    group_parity = lax.population_count(jnp.arange(groups, dtype=jnp.int32) & my_index) & 1
    parity = parity ^ group_parity[None, None, :, None]
    return (1 - 2 * parity).astype(jnp.bfloat16).reshape(OUTER, inner, groups * per_row)


def per_device(panel, signs, offsets):
    columns, length = panel.shape
    groups = lax.axis_size("ev")
    levels = groups.bit_length() - 1
    my_index = lax.axis_index("ev")
    inner = length // OUTER
    per_row = inner // STRIDE
    high = lax.Precision.HIGHEST

    signed = panel * signs.astype(jnp.bfloat16)[None, :]
    blocks = signed.reshape(columns, OUTER, inner)
    first = jnp.einsum(
        "xa,cab->xcb",
        hadamard(OUTER).astype(jnp.bfloat16),
        blocks,
        preferred_element_type=jnp.float32,
    )
    pick = selection(offsets, my_index, groups, inner)
    width = groups * per_row
    group = max(1, OUTER // width)
    count = OUTER // group
    lhs = first.reshape(count, group * columns, inner)
    rhs = pick.reshape(count, group, inner, width).transpose(0, 2, 1, 3).reshape(count, inner, group * width)
    wide = jnp.einsum(
        "gmb,gbn->gmn",
        lhs,
        rhs.astype(jnp.float32),
        precision=lax.Precision.HIGH,
        preferred_element_type=jnp.float32,
    ).reshape(count, group, columns, group, width)
    eye = (jnp.arange(group)[:, None] == jnp.arange(group)[None, :]).astype(jnp.float32)
    sampled = (wide * eye[None, :, None, :, None]).sum(axis=3).reshape(OUTER, columns, width)
    chunks = sampled.reshape(OUTER, columns, groups, per_row).transpose(2, 1, 0, 3)
    chunks = chunks.reshape(groups, columns, OUTER * per_row)
    own = lax.dynamic_index_in_dim(chunks, my_index, axis=0, keepdims=False)
    arrived = []
    for distance in range(1, groups):
        target = my_index ^ distance
        block = lax.dynamic_index_in_dim(chunks, target, axis=0, keepdims=False)
        pairs = [(source, source ^ distance) for source in range(groups)]
        arrived.append(lax.ppermute(block, "ev", pairs))
    chunks = own
    for block in arrived:
        chunks = chunks + block

    total_events = length * groups
    scale = 1.0 / math.sqrt(total_events * (total_events // STRIDE))
    sketch = chunks * scale
    partial_gram = jnp.dot(
        sketch,
        lax.all_gather(sketch, "col", axis=0, tiled=True).T,
        precision=high,
        preferred_element_type=jnp.float32,
    )
    for level in range(levels):
        partial_gram = partial_gram + exchange(partial_gram, "ev", level)
    return partial_gram


def solution(mesh):
    return jax.shard_map(
        per_device,
        mesh=mesh,
        in_specs=(P("col", "ev"), P("ev"), P()),
        out_specs=P("col", None),
        check_vma=False,
    )
```

```python
import math

import jax
import jax.numpy as jnp
from jax import lax
from jax.sharding import PartitionSpec as P

STRIDE = 64
OUTER = 128


def hadamard(order):
    index = jnp.arange(order, dtype=jnp.int32)
    both = index[:, None] & index[None, :]
    parity = jnp.zeros((order, order), jnp.int32)
    for level in range(order.bit_length() - 1):
        parity = parity + (both >> level & 1)
    return (1 - 2 * (parity % 2)).astype(jnp.float32)


def exchange(value, axis, bit):
    mask = 1 << bit
    pairs = [(source, source ^ mask) for source in range(lax.axis_size(axis))]
    return lax.ppermute(value, axis, pairs)


def group_sum(value, bits):
    groups = lax.axis_size("ev")
    my_index = lax.axis_index("ev")
    masks = [0]
    for bit in bits:
        masks = masks + [mask | (1 << bit) for mask in masks]
    values = [value]
    for mask in masks[1:]:
        pairs = [(source, source ^ mask) for source in range(groups)]
        values.append(lax.ppermute(value, "ev", pairs))
    mine = sum(((my_index >> bit) & 1) << place for place, bit in enumerate(bits))
    order = jnp.arange(len(masks), dtype=jnp.int32) ^ mine
    ordered = jnp.take(jnp.stack(values), order, axis=0)
    while ordered.shape[0] > 1:
        ordered = ordered[0::2] + ordered[1::2]
    return ordered[0]


def split3(value):
    hi = lax.reduce_precision(value, exponent_bits=8, mantissa_bits=7)
    rest = value - hi
    mid = lax.reduce_precision(rest, exponent_bits=8, mantissa_bits=7)
    low = rest - mid
    return tuple(piece.astype(jnp.bfloat16) for piece in (hi, mid, low))


def selection(offsets, my_index, groups, inner):
    per_row = inner // STRIDE
    off = offsets.reshape(groups, OUTER, per_row)
    rows = jnp.arange(per_row, dtype=jnp.int32)[None, None, :] * STRIDE + off
    rows = rows.transpose(1, 0, 2)
    lanes = jnp.arange(inner, dtype=jnp.int32)
    parity = lax.population_count(rows[:, None, :, :] & lanes[None, :, None, None]) & 1
    group_parity = lax.population_count(jnp.arange(groups, dtype=jnp.int32) & my_index) & 1
    parity = parity ^ group_parity[None, None, :, None]
    return (1 - 2 * parity).astype(jnp.bfloat16).reshape(OUTER, inner, groups * per_row)


def per_device(panel, signs, offsets):
    columns, length = panel.shape
    groups = lax.axis_size("ev")
    levels = groups.bit_length() - 1
    my_index = lax.axis_index("ev")
    inner = length // OUTER
    per_row = inner // STRIDE
    high = lax.Precision.HIGHEST

    signed = panel * signs.astype(jnp.bfloat16)[None, :]
    blocks = signed.reshape(columns, OUTER, inner)
    first = jnp.einsum(
        "xa,cab->xcb",
        hadamard(OUTER).astype(jnp.bfloat16),
        blocks,
        preferred_element_type=jnp.float32,
    )
    pick = selection(offsets, my_index, groups, inner)
    sampled = jnp.einsum(
        "xcb,xbj->xcj",
        first,
        pick.astype(jnp.float32),
        precision=lax.Precision.HIGH,
        preferred_element_type=jnp.float32,
    )
    chunks = sampled.reshape(OUTER, columns, groups, per_row).transpose(2, 1, 0, 3)
    chunks = chunks.reshape(groups, columns, OUTER * per_row)
    own = lax.dynamic_index_in_dim(chunks, my_index, axis=0, keepdims=False)
    arrived = []
    for distance in range(1, groups):
        target = my_index ^ distance
        block = lax.dynamic_index_in_dim(chunks, target, axis=0, keepdims=False)
        pairs = [(source, source ^ distance) for source in range(groups)]
        arrived.append(lax.ppermute(block, "ev", pairs))
    chunks = own
    for block in arrived:
        chunks = chunks + block

    total_events = length * groups
    scale = 1.0 / math.sqrt(total_events * (total_events // STRIDE))
    sketch = chunks * scale
    partial_gram = jnp.dot(
        sketch,
        lax.all_gather(sketch, "col", axis=0, tiled=True).T,
        precision=high,
        preferred_element_type=jnp.float32,
    )
    for start in range(0, levels, 2):
        partial_gram = group_sum(partial_gram, list(range(start, min(start + 2, levels))))
    return partial_gram


def solution(mesh):
    return jax.shard_map(
        per_device,
        mesh=mesh,
        in_specs=(P("col", "ev"), P("ev"), P()),
        out_specs=P("col", None),
        check_vma=False,
    )
```

```python
import math

import jax
import jax.numpy as jnp
from jax import lax
from jax.experimental import pallas as pl
from jax.sharding import PartitionSpec as P

STRIDE = 64
OUTER = 128


def hadamard(order):
    index = jnp.arange(order, dtype=jnp.int32)
    both = index[:, None] & index[None, :]
    parity = jnp.zeros((order, order), jnp.int32)
    for level in range(order.bit_length() - 1):
        parity = parity + (both >> level & 1)
    return (1 - 2 * (parity % 2)).astype(jnp.float32)


def exchange(value, axis, bit):
    mask = 1 << bit
    pairs = [(source, source ^ mask) for source in range(lax.axis_size(axis))]
    return lax.ppermute(value, axis, pairs)


def group_sum(value, bits):
    groups = lax.axis_size("ev")
    my_index = lax.axis_index("ev")
    masks = [0]
    for bit in bits:
        masks = masks + [mask | (1 << bit) for mask in masks]
    values = [value]
    for mask in masks[1:]:
        pairs = [(source, source ^ mask) for source in range(groups)]
        values.append(lax.ppermute(value, "ev", pairs))
    mine = sum(((my_index >> bit) & 1) << place for place, bit in enumerate(bits))
    order = jnp.arange(len(masks), dtype=jnp.int32) ^ mine
    ordered = jnp.take(jnp.stack(values), order, axis=0)
    while ordered.shape[0] > 1:
        ordered = ordered[0::2] + ordered[1::2]
    return ordered[0]


def factors(offsets, my_index, groups, length):
    inner = length // OUTER
    rows = STRIDE * jnp.arange(offsets.shape[0], dtype=jnp.int32) + offsets
    y = rows % inner
    x = rows % length // inner
    p = rows // length
    lanes = jnp.arange(inner, dtype=jnp.int32)[:, None]
    hy = 1 - 2 * (lax.population_count(y[None, :] & lanes) & 1)
    outer = jnp.arange(OUTER, dtype=jnp.int32)[:, None]
    parity = lax.population_count(x[None, :] & outer) + lax.population_count(p & my_index)[None, :]
    hx = 1 - 2 * (parity & 1)
    return hy.astype(jnp.bfloat16), hx.astype(jnp.float32)


def sketch_kernel(panel_ref, sign_ref, hy_ref, hx_ref, out_ref):
    block, samples = out_ref.shape
    inner = sign_ref.shape[1]
    rows = panel_ref[...].astype(jnp.float32).reshape(block, OUTER, inner) * sign_ref[...][None]
    rows = rows.reshape(block * OUTER, inner).astype(jnp.bfloat16)
    width = min(samples, 1024)
    for part in range(samples // width):
        lanes = pl.ds(part * width, width)
        mixed = jnp.dot(rows, hy_ref[:, lanes], preferred_element_type=jnp.float32)
        mixed = mixed.reshape(block, OUTER, width) * hx_ref[:, lanes][None]
        out_ref[:, lanes] = jnp.sum(mixed, axis=1)


def local_sketch(panel, sign, hy, hx):
    columns, length = panel.shape
    inner = length // OUTER
    samples = hy.shape[1]
    block = 8
    flops = 2 * columns * length * samples + 2 * columns * OUTER * samples
    return pl.pallas_call(
        sketch_kernel,
        out_shape=jax.ShapeDtypeStruct((columns, samples), jnp.float32),
        grid=(columns // block,),
        in_specs=[
            pl.BlockSpec((block * OUTER, inner), lambda i: (i, 0)),
            pl.BlockSpec((OUTER, inner), lambda i: (0, 0)),
            pl.BlockSpec((inner, samples), lambda i: (0, 0)),
            pl.BlockSpec((OUTER, samples), lambda i: (0, 0)),
        ],
        out_specs=pl.BlockSpec((block, samples), lambda i: (i, 0)),
        cost_estimate=pl.CostEstimate(
            flops=flops, transcendentals=0, bytes_accessed=columns * length * 2 + columns * samples * 4
        ),
    )(panel.reshape(columns * OUTER, inner), sign, hy, hx)


def per_device(panel, signs, offsets):
    columns, length = panel.shape
    groups = lax.axis_size("ev")
    levels = groups.bit_length() - 1
    my_index = lax.axis_index("ev")
    inner = length // OUTER
    per_row = inner // STRIDE
    high = lax.Precision.HIGHEST

    sign = signs.reshape(OUTER, inner).astype(jnp.float32)
    hy, hx = factors(offsets, my_index, groups, length)
    sampled = local_sketch(panel, sign, hy, hx)

    chunks = sampled.reshape(columns, groups, OUTER * per_row).transpose(1, 0, 2)
    own = lax.dynamic_index_in_dim(chunks, my_index, axis=0, keepdims=False)
    arrived = []
    for distance in range(1, groups):
        target = my_index ^ distance
        block = lax.dynamic_index_in_dim(chunks, target, axis=0, keepdims=False)
        pairs = [(source, source ^ distance) for source in range(groups)]
        arrived.append(lax.ppermute(block, "ev", pairs))
    chunks = own
    for block in arrived:
        chunks = chunks + block

    total_events = length * groups
    scale = 1.0 / math.sqrt(total_events * (total_events // STRIDE))
    sketch = chunks * scale
    partial_gram = jnp.dot(
        sketch,
        lax.all_gather(sketch, "col", axis=0, tiled=True).T,
        precision=high,
        preferred_element_type=jnp.float32,
    )
    for start in range(0, levels, 2):
        partial_gram = group_sum(partial_gram, list(range(start, min(start + 2, levels))))
    return partial_gram


def solution(mesh):
    return jax.shard_map(
        per_device,
        mesh=mesh,
        in_specs=(P("col", "ev"), P("ev"), P()),
        out_specs=P("col", None),
        check_vma=False,
    )
```

```python
import math

import jax
import jax.numpy as jnp
from jax import lax
from jax.experimental import pallas as pl
from jax.sharding import PartitionSpec as P

STRIDE = 64
OUTER = 128


def hadamard(order):
    index = jnp.arange(order, dtype=jnp.int32)
    both = index[:, None] & index[None, :]
    parity = jnp.zeros((order, order), jnp.int32)
    for level in range(order.bit_length() - 1):
        parity = parity + (both >> level & 1)
    return (1 - 2 * (parity % 2)).astype(jnp.float32)


def exchange(value, axis, bit):
    mask = 1 << bit
    pairs = [(source, source ^ mask) for source in range(lax.axis_size(axis))]
    return lax.ppermute(value, axis, pairs)


def group_sum(value, bits):
    groups = lax.axis_size("ev")
    my_index = lax.axis_index("ev")
    masks = [0]
    for bit in bits:
        masks = masks + [mask | (1 << bit) for mask in masks]
    values = [value]
    for mask in masks[1:]:
        pairs = [(source, source ^ mask) for source in range(groups)]
        values.append(lax.ppermute(value, "ev", pairs))
    mine = sum(((my_index >> bit) & 1) << place for place, bit in enumerate(bits))
    order = jnp.arange(len(masks), dtype=jnp.int32) ^ mine
    ordered = jnp.take(jnp.stack(values), order, axis=0)
    while ordered.shape[0] > 1:
        ordered = ordered[0::2] + ordered[1::2]
    return ordered[0]


def factors(offsets, my_index, groups, length):
    inner = length // OUTER
    rows = STRIDE * jnp.arange(offsets.shape[0], dtype=jnp.int32) + offsets
    y = rows % inner
    x = rows % length // inner
    p = rows // length
    lanes = jnp.arange(inner, dtype=jnp.int32)[:, None]
    hy = 1 - 2 * (lax.population_count(y[None, :] & lanes) & 1)
    outer = jnp.arange(OUTER, dtype=jnp.int32)[:, None]
    parity = lax.population_count(x[None, :] & outer) + lax.population_count(p & my_index)[None, :]
    hx = 1 - 2 * (parity & 1)
    return hy.astype(jnp.bfloat16), hx.astype(jnp.float32)


def sketch_kernel(panel_ref, sign_ref, hy_ref, hx_ref, out_ref):
    block, samples = out_ref.shape
    inner = hy_ref.shape[0]
    signed = panel_ref[...].astype(jnp.float32) * sign_ref[...]
    rows = jnp.concatenate(
        [signed[:, a * inner : (a + 1) * inner] for a in range(OUTER)], axis=0
    ).astype(jnp.bfloat16)
    width = min(samples, 1024)
    for part in range(samples // width):
        lanes = pl.ds(part * width, width)
        mixed = jnp.dot(rows, hy_ref[:, lanes], preferred_element_type=jnp.float32)
        mixed = mixed.reshape(OUTER, block, width) * hx_ref[:, lanes][:, None, :]
        out_ref[:, lanes] = jnp.sum(mixed, axis=0)


def local_sketch(panel, sign, hy, hx):
    columns, length = panel.shape
    samples = hy.shape[1]
    block = 8
    flops = 2 * columns * length * samples + 2 * columns * OUTER * samples
    return pl.pallas_call(
        sketch_kernel,
        out_shape=jax.ShapeDtypeStruct((columns, samples), jnp.float32),
        grid=(columns // block,),
        in_specs=[
            pl.BlockSpec((block, length), lambda i: (i, 0)),
            pl.BlockSpec((1, length), lambda i: (0, 0)),
            pl.BlockSpec(hy.shape, lambda i: (0, 0)),
            pl.BlockSpec(hx.shape, lambda i: (0, 0)),
        ],
        out_specs=pl.BlockSpec((block, samples), lambda i: (i, 0)),
        cost_estimate=pl.CostEstimate(
            flops=flops, transcendentals=0, bytes_accessed=columns * length * 2 + columns * samples * 4
        ),
    )(panel, sign, hy, hx)


def per_device(panel, signs, offsets):
    columns, length = panel.shape
    groups = lax.axis_size("ev")
    levels = groups.bit_length() - 1
    my_index = lax.axis_index("ev")
    inner = length // OUTER
    per_row = inner // STRIDE
    high = lax.Precision.HIGHEST

    sign = signs.reshape(1, length).astype(jnp.float32)
    hy, hx = factors(offsets, my_index, groups, length)
    sampled = local_sketch(panel, sign, hy, hx)

    chunks = sampled.reshape(columns, groups, OUTER * per_row).transpose(1, 0, 2)
    own = lax.dynamic_index_in_dim(chunks, my_index, axis=0, keepdims=False)
    arrived = []
    for distance in range(1, groups):
        target = my_index ^ distance
        block = lax.dynamic_index_in_dim(chunks, target, axis=0, keepdims=False)
        pairs = [(source, source ^ distance) for source in range(groups)]
        arrived.append(lax.ppermute(block, "ev", pairs))
    chunks = own
    for block in arrived:
        chunks = chunks + block

    total_events = length * groups
    scale = 1.0 / math.sqrt(total_events * (total_events // STRIDE))
    sketch = chunks * scale
    partial_gram = jnp.dot(
        sketch,
        lax.all_gather(sketch, "col", axis=0, tiled=True).T,
        precision=high,
        preferred_element_type=jnp.float32,
    )
    for start in range(0, levels, 2):
        partial_gram = group_sum(partial_gram, list(range(start, min(start + 2, levels))))
    return partial_gram


def solution(mesh):
    return jax.shard_map(
        per_device,
        mesh=mesh,
        in_specs=(P("col", "ev"), P("ev"), P()),
        out_specs=P("col", None),
        check_vma=False,
    )
```

```python
import math

import jax
import jax.numpy as jnp
from jax import lax
from jax.sharding import PartitionSpec as P

STRIDE = 64
OUTER = 128


def hadamard(order):
    index = jnp.arange(order, dtype=jnp.int32)
    both = index[:, None] & index[None, :]
    parity = jnp.zeros((order, order), jnp.int32)
    for level in range(order.bit_length() - 1):
        parity = parity + (both >> level & 1)
    return (1 - 2 * (parity % 2)).astype(jnp.float32)


def exchange(value, axis, bit):
    mask = 1 << bit
    pairs = [(source, source ^ mask) for source in range(lax.axis_size(axis))]
    return lax.ppermute(value, axis, pairs)


def group_sum(value, bits):
    groups = lax.axis_size("ev")
    my_index = lax.axis_index("ev")
    masks = [0]
    for bit in bits:
        masks = masks + [mask | (1 << bit) for mask in masks]
    values = [value]
    for mask in masks[1:]:
        pairs = [(source, source ^ mask) for source in range(groups)]
        values.append(lax.ppermute(value, "ev", pairs))
    mine = sum(((my_index >> bit) & 1) << place for place, bit in enumerate(bits))
    order = jnp.arange(len(masks), dtype=jnp.int32) ^ mine
    ordered = jnp.take(jnp.stack(values), order, axis=0)
    while ordered.shape[0] > 1:
        ordered = ordered[0::2] + ordered[1::2]
    return ordered[0]


def per_device(panel, signs, offsets):
    columns, length = panel.shape
    groups = lax.axis_size("ev")
    levels = groups.bit_length() - 1
    my_index = lax.axis_index("ev")
    inner = length // OUTER
    per_row = inner // STRIDE
    high = lax.Precision.HIGHEST

    signed = jnp.where(signs[None, :] > 0, panel, -panel)
    events = signed.reshape(columns, OUTER, inner).transpose(2, 1, 0).reshape(inner, OUTER * columns)
    mixed = jnp.dot(
        hadamard(inner).astype(jnp.bfloat16), events, preferred_element_type=jnp.float32
    ).reshape(inner, OUTER, columns)
    full = jnp.einsum(
        "xa,yac->yxc", hadamard(OUTER), mixed, precision=lax.Precision.HIGH,
        preferred_element_type=jnp.float32,
    ).reshape(inner * OUTER, columns)
    rows = STRIDE * jnp.arange(offsets.shape[0], dtype=jnp.int32) + offsets
    spot = rows % inner * OUTER + rows % length // inner
    flip = (1 - 2 * (lax.population_count(rows // length & my_index) & 1)).astype(jnp.float32)
    sampled = (jnp.take(full, spot, axis=0) * flip[:, None]).T

    chunks = sampled.reshape(columns, groups, OUTER * per_row).transpose(1, 0, 2)
    own = lax.dynamic_index_in_dim(chunks, my_index, axis=0, keepdims=False)
    arrived = []
    for distance in range(1, groups):
        target = my_index ^ distance
        block = lax.dynamic_index_in_dim(chunks, target, axis=0, keepdims=False)
        pairs = [(source, source ^ distance) for source in range(groups)]
        arrived.append(lax.ppermute(block, "ev", pairs))
    chunks = own
    for block in arrived:
        chunks = chunks + block

    total_events = length * groups
    scale = 1.0 / math.sqrt(total_events * (total_events // STRIDE))
    sketch = chunks * scale
    partial_gram = jnp.dot(
        sketch,
        lax.all_gather(sketch, "col", axis=0, tiled=True).T,
        precision=high,
        preferred_element_type=jnp.float32,
    )
    for start in range(0, levels, 2):
        partial_gram = group_sum(partial_gram, list(range(start, min(start + 2, levels))))
    return partial_gram


def solution(mesh):
    return jax.shard_map(
        per_device,
        mesh=mesh,
        in_specs=(P("col", "ev"), P("ev"), P()),
        out_specs=P("col", None),
        check_vma=False,
    )
```

```python
import math

import jax
import jax.numpy as jnp
from jax import lax
from jax.sharding import PartitionSpec as P

STRIDE = 64
OUTER = 128


def hadamard(order):
    index = jnp.arange(order, dtype=jnp.int32)
    both = index[:, None] & index[None, :]
    parity = jnp.zeros((order, order), jnp.int32)
    for level in range(order.bit_length() - 1):
        parity = parity + (both >> level & 1)
    return (1 - 2 * (parity % 2)).astype(jnp.float32)


def exchange(value, axis, bit):
    mask = 1 << bit
    pairs = [(source, source ^ mask) for source in range(lax.axis_size(axis))]
    return lax.ppermute(value, axis, pairs)


def group_sum(value, bits):
    groups = lax.axis_size("ev")
    masks = [0]
    for bit in bits:
        masks = masks + [mask | (1 << bit) for mask in masks]
    values = [value]
    for mask in masks[1:]:
        pairs = [(source, source ^ mask) for source in range(groups)]
        values.append(lax.ppermute(value, "ev", pairs))
    while len(values) > 1:
        values = [values[i] + values[i + 1] for i in range(0, len(values), 2)]
    return values[0]


def split3(value):
    hi = lax.reduce_precision(value, exponent_bits=8, mantissa_bits=7)
    rest = value - hi
    mid = lax.reduce_precision(rest, exponent_bits=8, mantissa_bits=7)
    low = rest - mid
    return tuple(piece.astype(jnp.bfloat16) for piece in (hi, mid, low))


def selection(offsets, my_index, groups, inner):
    per_row = inner // STRIDE
    off = offsets.reshape(groups, OUTER, per_row)
    rows = jnp.arange(per_row, dtype=jnp.int32)[None, None, :] * STRIDE + off
    rows = rows.transpose(1, 0, 2)
    lanes = jnp.arange(inner, dtype=jnp.int32)
    parity = lax.population_count(rows[:, None, :, :] & lanes[None, :, None, None]) & 1
    group_parity = lax.population_count(jnp.arange(groups, dtype=jnp.int32) & my_index) & 1
    parity = parity ^ group_parity[None, None, :, None]
    return (1 - 2 * parity).astype(jnp.bfloat16).reshape(OUTER, inner, groups * per_row)


def per_device(panel, signs, offsets):
    columns, length = panel.shape
    groups = lax.axis_size("ev")
    levels = groups.bit_length() - 1
    my_index = lax.axis_index("ev")
    inner = length // OUTER
    per_row = inner // STRIDE
    high = lax.Precision.HIGHEST

    signed = panel * signs.astype(jnp.bfloat16)[None, :]
    blocks = signed.reshape(columns, OUTER, inner)
    first = jnp.einsum(
        "xa,cab->xcb",
        hadamard(OUTER).astype(jnp.bfloat16),
        blocks,
        preferred_element_type=jnp.float32,
    )
    pick = selection(offsets, my_index, groups, inner)
    sampled = jnp.einsum(
        "xcb,xbj->xcj",
        first,
        pick.astype(jnp.float32),
        precision=lax.Precision.HIGH,
        preferred_element_type=jnp.float32,
    )
    chunks = sampled.reshape(OUTER, columns, groups, per_row).transpose(2, 1, 0, 3)
    chunks = chunks.reshape(groups, columns, OUTER * per_row)
    own = lax.dynamic_index_in_dim(chunks, my_index, axis=0, keepdims=False)
    arrived = []
    for distance in range(1, groups):
        target = my_index ^ distance
        block = lax.dynamic_index_in_dim(chunks, target, axis=0, keepdims=False)
        pairs = [(source, source ^ distance) for source in range(groups)]
        arrived.append(lax.ppermute(block, "ev", pairs))
    chunks = own
    for block in arrived:
        chunks = chunks + block

    total_events = length * groups
    scale = 1.0 / math.sqrt(total_events * (total_events // STRIDE))
    sketch = chunks * scale
    partial_gram = jnp.dot(
        sketch,
        lax.all_gather(sketch, "col", axis=0, tiled=True).T,
        precision=high,
        preferred_element_type=jnp.float32,
    )
    for start in range(0, levels, 2):
        partial_gram = group_sum(partial_gram, list(range(start, min(start + 2, levels))))
    return partial_gram


def solution(mesh):
    return jax.shard_map(
        per_device,
        mesh=mesh,
        in_specs=(P("col", "ev"), P("ev"), P()),
        out_specs=P("col", None),
        check_vma=False,
    )
```

```python
import math

import jax
import jax.numpy as jnp
from jax import lax
from jax.sharding import PartitionSpec as P

STRIDE = 64
OUTER = 128


def hadamard(order):
    index = jnp.arange(order, dtype=jnp.int32)
    both = index[:, None] & index[None, :]
    parity = jnp.zeros((order, order), jnp.int32)
    for level in range(order.bit_length() - 1):
        parity = parity + (both >> level & 1)
    return (1 - 2 * (parity % 2)).astype(jnp.float32)


def exchange(value, axis, bit):
    mask = 1 << bit
    pairs = [(source, source ^ mask) for source in range(lax.axis_size(axis))]
    return lax.ppermute(value, axis, pairs)


def group_sum(value, bits):
    groups = lax.axis_size("ev")
    masks = [0]
    for bit in bits:
        masks = masks + [mask | (1 << bit) for mask in masks]
    values = [value]
    for mask in masks[1:]:
        pairs = [(source, source ^ mask) for source in range(groups)]
        values.append(lax.ppermute(value, "ev", pairs))
    while len(values) > 1:
        values = [values[i] + values[i + 1] for i in range(0, len(values), 2)]
    return values[0]


def split3(value):
    hi = lax.reduce_precision(value, exponent_bits=8, mantissa_bits=7)
    rest = value - hi
    mid = lax.reduce_precision(rest, exponent_bits=8, mantissa_bits=7)
    low = rest - mid
    return tuple(piece.astype(jnp.bfloat16) for piece in (hi, mid, low))


def selection(offsets, my_index, groups, inner):
    per_row = inner // STRIDE
    off = offsets.reshape(groups, OUTER, per_row)
    rows = jnp.arange(per_row, dtype=jnp.int32)[None, None, :] * STRIDE + off
    rows = rows.transpose(1, 0, 2)
    lanes = jnp.arange(inner, dtype=jnp.int32)
    parity = lax.population_count(rows[:, None, :, :] & lanes[None, :, None, None]) & 1
    group_parity = lax.population_count(jnp.arange(groups, dtype=jnp.int32) & my_index) & 1
    parity = parity ^ group_parity[None, None, :, None]
    return (1 - 2 * parity).astype(jnp.bfloat16).reshape(OUTER, inner, groups * per_row)


def per_device(panel, signs, offsets):
    columns, length = panel.shape
    groups = lax.axis_size("ev")
    levels = groups.bit_length() - 1
    my_index = lax.axis_index("ev")
    inner = length // OUTER
    per_row = inner // STRIDE
    high = lax.Precision.HIGHEST

    signed = panel * signs.astype(jnp.bfloat16)[None, :]
    blocks = signed.reshape(columns, OUTER, inner)
    first = jnp.einsum(
        "xa,cab->xcb",
        hadamard(OUTER).astype(jnp.bfloat16),
        blocks,
        preferred_element_type=jnp.float32,
    )
    pick = selection(offsets, my_index, groups, inner)
    sampled = jnp.einsum(
        "xcb,xbj->xcj",
        first,
        pick.astype(jnp.float32),
        precision=lax.Precision.HIGH,
        preferred_element_type=jnp.float32,
    )
    chunks = sampled.reshape(OUTER, columns, groups, per_row).transpose(2, 1, 0, 3)
    chunks = chunks.reshape(groups, columns, OUTER * per_row)
    own = lax.dynamic_index_in_dim(chunks, my_index, axis=0, keepdims=False)
    arrived = []
    for distance in range(1, groups):
        target = my_index ^ distance
        block = lax.dynamic_index_in_dim(chunks, target, axis=0, keepdims=False)
        pairs = [(source, source ^ distance) for source in range(groups)]
        arrived.append(lax.ppermute(block, "ev", pairs))
    chunks = own
    for block in arrived:
        chunks = chunks + block

    total_events = length * groups
    scale = 1.0 / math.sqrt(total_events * (total_events // STRIDE))
    sketch = chunks * scale
    partial_gram = jnp.dot(
        sketch,
        lax.all_gather(sketch, "col", axis=0, tiled=True).T,
        precision=high,
        preferred_element_type=jnp.float32,
    )
    for start in range(1, levels, 2):
        partial_gram = group_sum(partial_gram, list(range(start, min(start + 2, levels))))
    partial_gram = group_sum(partial_gram, [0])
    return partial_gram


def solution(mesh):
    return jax.shard_map(
        per_device,
        mesh=mesh,
        in_specs=(P("col", "ev"), P("ev"), P()),
        out_specs=P("col", None),
        check_vma=False,
    )
```

```python
import math

import jax
import jax.numpy as jnp
from jax import lax
from jax.experimental import pallas as pl
from jax.sharding import PartitionSpec as P

STRIDE = 64
OUTER = 128


def hadamard(order):
    index = jnp.arange(order, dtype=jnp.int32)
    both = index[:, None] & index[None, :]
    parity = jnp.zeros((order, order), jnp.int32)
    for level in range(order.bit_length() - 1):
        parity = parity + (both >> level & 1)
    return (1 - 2 * (parity % 2)).astype(jnp.float32)


def exchange(value, axis, bit):
    mask = 1 << bit
    pairs = [(source, source ^ mask) for source in range(lax.axis_size(axis))]
    return lax.ppermute(value, axis, pairs)


def group_sum(value, bits):
    groups = lax.axis_size("ev")
    masks = [0]
    for bit in bits:
        masks = masks + [mask | (1 << bit) for mask in masks]
    values = [value]
    for mask in masks[1:]:
        pairs = [(source, source ^ mask) for source in range(groups)]
        values.append(lax.ppermute(value, "ev", pairs))
    while len(values) > 1:
        values = [values[i] + values[i + 1] for i in range(0, len(values), 2)]
    return values[0]


def factors(offsets, my_index, groups, length):
    inner = length // OUTER
    rows = STRIDE * jnp.arange(offsets.shape[0], dtype=jnp.int32) + offsets
    y = rows % inner
    x = rows % length // inner
    p = rows // length
    lanes = jnp.arange(inner, dtype=jnp.int32)[:, None]
    hy = 1 - 2 * (lax.population_count(y[None, :] & lanes) & 1)
    outer = jnp.arange(OUTER, dtype=jnp.int32)[:, None]
    parity = lax.population_count(x[None, :] & outer) + lax.population_count(p & my_index)[None, :]
    hx = 1 - 2 * (parity & 1)
    return hy.astype(jnp.bfloat16), hx.astype(jnp.float32)


def sketch_kernel(panel_ref, sign_ref, hy_ref, hx_ref, out_ref):
    groups, block, chunk = out_ref.shape
    inner = hy_ref.shape[0]
    samples = hy_ref.shape[1]
    signed = panel_ref[...].astype(jnp.float32) * sign_ref[...].astype(jnp.float32)
    rows = jnp.concatenate(
        [signed[:, a * inner : (a + 1) * inner] for a in range(OUTER)], axis=0
    ).astype(jnp.bfloat16)
    width = min(samples, 512)
    for part in range(samples // width):
        lanes = pl.ds(part * width, width)
        mixed = jnp.dot(rows, hy_ref[:, lanes], preferred_element_type=jnp.float32)
        mixed = mixed.reshape(OUTER, block, width) * hx_ref[:, lanes][:, None, :]
        total = jnp.sum(mixed, axis=0)
        for piece in range(width // chunk):
            out_ref[(part * width) // chunk + piece] = total[:, piece * chunk : (piece + 1) * chunk]


def local_sketch(panel, sign, hy, hx, groups):
    columns, length = panel.shape
    samples = hy.shape[1]
    chunk = samples // groups
    block = 16
    flops = 2 * columns * length * samples + 2 * columns * OUTER * samples
    return pl.pallas_call(
        sketch_kernel,
        out_shape=jax.ShapeDtypeStruct((groups, columns, chunk), jnp.float32),
        grid=(columns // block,),
        in_specs=[
            pl.BlockSpec((block, length), lambda i: (i, 0)),
            pl.BlockSpec((1, length), lambda i: (0, 0)),
            pl.BlockSpec(hy.shape, lambda i: (0, 0)),
            pl.BlockSpec(hx.shape, lambda i: (0, 0)),
        ],
        out_specs=pl.BlockSpec((groups, block, chunk), lambda i: (0, i, 0)),
        cost_estimate=pl.CostEstimate(
            flops=flops, transcendentals=0, bytes_accessed=columns * length * 2 + columns * samples * 4
        ),
    )(panel, sign, hy, hx)


def per_device(panel, signs, offsets):
    columns, length = panel.shape
    groups = lax.axis_size("ev")
    levels = groups.bit_length() - 1
    my_index = lax.axis_index("ev")
    inner = length // OUTER
    per_row = inner // STRIDE
    high = lax.Precision.HIGHEST

    sign = signs.reshape(1, length)
    hy, hx = factors(offsets, my_index, groups, length)
    chunks = local_sketch(panel, sign, hy, hx, groups)
    own = lax.dynamic_index_in_dim(chunks, my_index, axis=0, keepdims=False)
    arrived = []
    for distance in range(1, groups):
        target = my_index ^ distance
        block = lax.dynamic_index_in_dim(chunks, target, axis=0, keepdims=False)
        pairs = [(source, source ^ distance) for source in range(groups)]
        arrived.append(lax.ppermute(block, "ev", pairs))
    chunks = own
    for block in arrived:
        chunks = chunks + block

    total_events = length * groups
    scale = 1.0 / math.sqrt(total_events * (total_events // STRIDE))
    sketch = chunks * scale
    partial_gram = jnp.dot(
        sketch,
        lax.all_gather(sketch, "col", axis=0, tiled=True).T,
        precision=high,
        preferred_element_type=jnp.float32,
    )
    for start in range(0, levels, 2):
        partial_gram = group_sum(partial_gram, list(range(start, min(start + 2, levels))))
    return partial_gram


def solution(mesh):
    return jax.shard_map(
        per_device,
        mesh=mesh,
        in_specs=(P("col", "ev"), P("ev"), P()),
        out_specs=P("col", None),
        check_vma=False,
    )
```

```python
import math

import jax
import jax.numpy as jnp
from jax import lax
from jax.experimental import pallas as pl
from jax.sharding import PartitionSpec as P

STRIDE = 64
OUTER = 128


def hadamard(order):
    index = jnp.arange(order, dtype=jnp.int32)
    both = index[:, None] & index[None, :]
    parity = jnp.zeros((order, order), jnp.int32)
    for level in range(order.bit_length() - 1):
        parity = parity + (both >> level & 1)
    return (1 - 2 * (parity % 2)).astype(jnp.float32)


def exchange(value, axis, bit):
    mask = 1 << bit
    pairs = [(source, source ^ mask) for source in range(lax.axis_size(axis))]
    return lax.ppermute(value, axis, pairs)


def group_sum(value, bits):
    groups = lax.axis_size("ev")
    masks = [0]
    for bit in bits:
        masks = masks + [mask | (1 << bit) for mask in masks]
    values = [value]
    for mask in masks[1:]:
        pairs = [(source, source ^ mask) for source in range(groups)]
        values.append(lax.ppermute(value, "ev", pairs))
    while len(values) > 1:
        values = [values[i] + values[i + 1] for i in range(0, len(values), 2)]
    return values[0]


def gather_kernel(full_ref, index_ref, out_ref):
    out_ref[...] = jnp.take_along_axis(full_ref[...], index_ref[...], axis=1)


def pick_lanes(full, index):
    rows, lanes = full.shape
    block = 1024
    tiled = jnp.tile(index, (block // index.shape[0], 1))
    return pl.pallas_call(
        gather_kernel,
        out_shape=jax.ShapeDtypeStruct((rows, lanes), full.dtype),
        grid=(rows // block,),
        in_specs=[
            pl.BlockSpec((block, lanes), lambda i: (i, 0)),
            pl.BlockSpec((block, lanes), lambda i: (0, 0)),
        ],
        out_specs=pl.BlockSpec((block, lanes), lambda i: (i, 0)),
    )(full, tiled)


def per_device(panel, signs, offsets):
    columns, length = panel.shape
    groups = lax.axis_size("ev")
    levels = groups.bit_length() - 1
    my_index = lax.axis_index("ev")
    inner = length // OUTER
    per_row = inner // STRIDE
    high = lax.Precision.HIGHEST

    signed = panel * signs.astype(jnp.bfloat16)[None, :]
    blocks = signed.reshape(columns, OUTER, inner)
    first = jnp.einsum(
        "xa,cab->cxb",
        hadamard(OUTER).astype(jnp.bfloat16),
        blocks,
        preferred_element_type=jnp.float32,
    )
    full = jnp.dot(
        first.reshape(columns * OUTER, inner),
        hadamard(inner),
        precision=lax.Precision.HIGH,
        preferred_element_type=jnp.float32,
    )
    width = groups * per_row
    off = offsets.reshape(groups, OUTER, per_row).transpose(1, 0, 2)
    wanted = (jnp.arange(per_row, dtype=jnp.int32)[None, None, :] * STRIDE + off).reshape(OUTER, width)
    wanted = jnp.pad(wanted, ((0, 0), (0, inner - width)))
    picked = pick_lanes(full, wanted).reshape(columns, OUTER, inner)[:, :, :width]
    flip = (1 - 2 * (lax.population_count(jnp.arange(groups, dtype=jnp.int32) & my_index) & 1)).astype(jnp.float32)
    picked = picked.reshape(columns, OUTER, groups, per_row) * flip[None, None, :, None]
    chunks = picked.transpose(2, 0, 1, 3).reshape(groups, columns, OUTER * per_row)
    own = lax.dynamic_index_in_dim(chunks, my_index, axis=0, keepdims=False)
    arrived = []
    for distance in range(1, groups):
        target = my_index ^ distance
        block = lax.dynamic_index_in_dim(chunks, target, axis=0, keepdims=False)
        pairs = [(source, source ^ distance) for source in range(groups)]
        arrived.append(lax.ppermute(block, "ev", pairs))
    chunks = own
    for block in arrived:
        chunks = chunks + block

    total_events = length * groups
    scale = 1.0 / math.sqrt(total_events * (total_events // STRIDE))
    sketch = chunks * scale
    partial_gram = jnp.dot(
        sketch,
        lax.all_gather(sketch, "col", axis=0, tiled=True).T,
        precision=high,
        preferred_element_type=jnp.float32,
    )
    for start in range(0, levels, 2):
        partial_gram = group_sum(partial_gram, list(range(start, min(start + 2, levels))))
    return partial_gram


def solution(mesh):
    return jax.shard_map(
        per_device,
        mesh=mesh,
        in_specs=(P("col", "ev"), P("ev"), P()),
        out_specs=P("col", None),
        check_vma=False,
    )
```

```python
import math

import jax
import jax.numpy as jnp
from jax import lax
from jax.sharding import PartitionSpec as P

STRIDE = 64
OUTER = 128


def hadamard(order):
    index = jnp.arange(order, dtype=jnp.int32)
    both = index[:, None] & index[None, :]
    parity = jnp.zeros((order, order), jnp.int32)
    for level in range(order.bit_length() - 1):
        parity = parity + (both >> level & 1)
    return (1 - 2 * (parity % 2)).astype(jnp.float32)


def exchange(value, axis, bit):
    mask = 1 << bit
    pairs = [(source, source ^ mask) for source in range(lax.axis_size(axis))]
    return lax.ppermute(value, axis, pairs)


def group_sum(value, bits):
    groups = lax.axis_size("ev")
    masks = [0]
    for bit in bits:
        masks = masks + [mask | (1 << bit) for mask in masks]
    values = [value]
    for mask in masks[1:]:
        pairs = [(source, source ^ mask) for source in range(groups)]
        values.append(lax.ppermute(value, "ev", pairs))
    while len(values) > 1:
        values = [values[i] + values[i + 1] for i in range(0, len(values), 2)]
    return values[0]


def split3(value):
    hi = lax.reduce_precision(value, exponent_bits=8, mantissa_bits=7)
    rest = value - hi
    mid = lax.reduce_precision(rest, exponent_bits=8, mantissa_bits=7)
    low = rest - mid
    return tuple(piece.astype(jnp.bfloat16) for piece in (hi, mid, low))


def selection(offsets, my_index, groups, inner):
    per_row = inner // STRIDE
    off = offsets.reshape(groups, OUTER, per_row)
    rows = jnp.arange(per_row, dtype=jnp.int32)[None, None, :] * STRIDE + off
    rows = rows.transpose(1, 0, 2)
    lanes = jnp.arange(inner, dtype=jnp.int32)
    parity = lax.population_count(rows[:, None, :, :] & lanes[None, :, None, None]) & 1
    group_parity = lax.population_count(jnp.arange(groups, dtype=jnp.int32) & my_index) & 1
    parity = parity ^ group_parity[None, None, :, None]
    return (1 - 2 * parity).astype(jnp.bfloat16).reshape(OUTER, inner, groups * per_row)


def per_device(panel, signs, offsets):
    columns, length = panel.shape
    groups = lax.axis_size("ev")
    levels = groups.bit_length() - 1
    my_index = lax.axis_index("ev")
    inner = length // OUTER
    per_row = inner // STRIDE
    high = lax.Precision.HIGHEST

    signed = panel * signs.astype(jnp.bfloat16)[None, :]
    blocks = signed.reshape(columns, OUTER, inner)
    first = jnp.einsum(
        "xa,cab->cxb",
        hadamard(OUTER).astype(jnp.bfloat16),
        blocks,
        preferred_element_type=jnp.float32,
    )
    pick = selection(offsets, my_index, groups, inner)
    sampled = jnp.einsum(
        "cxb,xbj->xcj",
        first,
        pick.astype(jnp.float32),
        precision=lax.Precision.HIGH,
        preferred_element_type=jnp.float32,
    )
    chunks = sampled.reshape(OUTER, columns, groups, per_row).transpose(2, 1, 0, 3)
    chunks = chunks.reshape(groups, columns, OUTER * per_row)
    own = lax.dynamic_index_in_dim(chunks, my_index, axis=0, keepdims=False)
    arrived = []
    for distance in range(1, groups):
        target = my_index ^ distance
        block = lax.dynamic_index_in_dim(chunks, target, axis=0, keepdims=False)
        pairs = [(source, source ^ distance) for source in range(groups)]
        arrived.append(lax.ppermute(block, "ev", pairs))
    chunks = own
    for block in arrived:
        chunks = chunks + block

    total_events = length * groups
    scale = 1.0 / math.sqrt(total_events * (total_events // STRIDE))
    sketch = chunks * scale
    partial_gram = jnp.dot(
        sketch,
        lax.all_gather(sketch, "col", axis=0, tiled=True).T,
        precision=high,
        preferred_element_type=jnp.float32,
    )
    for start in range(0, levels, 2):
        partial_gram = group_sum(partial_gram, list(range(start, min(start + 2, levels))))
    return partial_gram


def solution(mesh):
    return jax.shard_map(
        per_device,
        mesh=mesh,
        in_specs=(P("col", "ev"), P("ev"), P()),
        out_specs=P("col", None),
        check_vma=False,
    )
```

```python
import math

import jax
import jax.numpy as jnp
from jax import lax
from jax.sharding import PartitionSpec as P

STRIDE = 64
OUTER = 64


def hadamard(order):
    index = jnp.arange(order, dtype=jnp.int32)
    both = index[:, None] & index[None, :]
    parity = jnp.zeros((order, order), jnp.int32)
    for level in range(order.bit_length() - 1):
        parity = parity + (both >> level & 1)
    return (1 - 2 * (parity % 2)).astype(jnp.float32)


def exchange(value, axis, bit):
    mask = 1 << bit
    pairs = [(source, source ^ mask) for source in range(lax.axis_size(axis))]
    return lax.ppermute(value, axis, pairs)


def group_sum(value, bits):
    groups = lax.axis_size("ev")
    masks = [0]
    for bit in bits:
        masks = masks + [mask | (1 << bit) for mask in masks]
    values = [value]
    for mask in masks[1:]:
        pairs = [(source, source ^ mask) for source in range(groups)]
        values.append(lax.ppermute(value, "ev", pairs))
    while len(values) > 1:
        values = [values[i] + values[i + 1] for i in range(0, len(values), 2)]
    return values[0]


def split3(value):
    hi = lax.reduce_precision(value, exponent_bits=8, mantissa_bits=7)
    rest = value - hi
    mid = lax.reduce_precision(rest, exponent_bits=8, mantissa_bits=7)
    low = rest - mid
    return tuple(piece.astype(jnp.bfloat16) for piece in (hi, mid, low))


def selection(offsets, my_index, groups, inner):
    per_row = inner // STRIDE
    off = offsets.reshape(groups, OUTER, per_row)
    rows = jnp.arange(per_row, dtype=jnp.int32)[None, None, :] * STRIDE + off
    rows = rows.transpose(1, 0, 2)
    lanes = jnp.arange(inner, dtype=jnp.int32)
    parity = lax.population_count(rows[:, None, :, :] & lanes[None, :, None, None]) & 1
    group_parity = lax.population_count(jnp.arange(groups, dtype=jnp.int32) & my_index) & 1
    parity = parity ^ group_parity[None, None, :, None]
    return (1 - 2 * parity).astype(jnp.bfloat16).reshape(OUTER, inner, groups * per_row)


def per_device(panel, signs, offsets):
    columns, length = panel.shape
    groups = lax.axis_size("ev")
    levels = groups.bit_length() - 1
    my_index = lax.axis_index("ev")
    inner = length // OUTER
    per_row = inner // STRIDE
    high = lax.Precision.HIGHEST

    signed = panel * signs.astype(jnp.bfloat16)[None, :]
    blocks = signed.reshape(columns, OUTER, inner)
    first = jnp.einsum(
        "xa,cab->xcb",
        hadamard(OUTER).astype(jnp.bfloat16),
        blocks,
        preferred_element_type=jnp.float32,
    )
    pick = selection(offsets, my_index, groups, inner)
    sampled = jnp.einsum(
        "xcb,xbj->xcj",
        first,
        pick.astype(jnp.float32),
        precision=lax.Precision.HIGH,
        preferred_element_type=jnp.float32,
    )
    chunks = sampled.reshape(OUTER, columns, groups, per_row).transpose(2, 1, 0, 3)
    chunks = chunks.reshape(groups, columns, OUTER * per_row)
    own = lax.dynamic_index_in_dim(chunks, my_index, axis=0, keepdims=False)
    arrived = []
    for distance in range(1, groups):
        target = my_index ^ distance
        block = lax.dynamic_index_in_dim(chunks, target, axis=0, keepdims=False)
        pairs = [(source, source ^ distance) for source in range(groups)]
        arrived.append(lax.ppermute(block, "ev", pairs))
    chunks = own
    for block in arrived:
        chunks = chunks + block

    total_events = length * groups
    scale = 1.0 / math.sqrt(total_events * (total_events // STRIDE))
    sketch = chunks * scale
    partial_gram = jnp.dot(
        sketch,
        lax.all_gather(sketch, "col", axis=0, tiled=True).T,
        precision=high,
        preferred_element_type=jnp.float32,
    )
    for start in range(0, levels, 2):
        partial_gram = group_sum(partial_gram, list(range(start, min(start + 2, levels))))
    return partial_gram


def solution(mesh):
    return jax.shard_map(
        per_device,
        mesh=mesh,
        in_specs=(P("col", "ev"), P("ev"), P()),
        out_specs=P("col", None),
        check_vma=False,
    )
```

```python
import math

import jax
import jax.numpy as jnp
from jax import lax
from jax.sharding import PartitionSpec as P

STRIDE = 64
OUTER = 32


def hadamard(order):
    index = jnp.arange(order, dtype=jnp.int32)
    both = index[:, None] & index[None, :]
    parity = jnp.zeros((order, order), jnp.int32)
    for level in range(order.bit_length() - 1):
        parity = parity + (both >> level & 1)
    return (1 - 2 * (parity % 2)).astype(jnp.float32)


def exchange(value, axis, bit):
    mask = 1 << bit
    pairs = [(source, source ^ mask) for source in range(lax.axis_size(axis))]
    return lax.ppermute(value, axis, pairs)


def group_sum(value, bits):
    groups = lax.axis_size("ev")
    masks = [0]
    for bit in bits:
        masks = masks + [mask | (1 << bit) for mask in masks]
    values = [value]
    for mask in masks[1:]:
        pairs = [(source, source ^ mask) for source in range(groups)]
        values.append(lax.ppermute(value, "ev", pairs))
    while len(values) > 1:
        values = [values[i] + values[i + 1] for i in range(0, len(values), 2)]
    return values[0]


def split3(value):
    hi = lax.reduce_precision(value, exponent_bits=8, mantissa_bits=7)
    rest = value - hi
    mid = lax.reduce_precision(rest, exponent_bits=8, mantissa_bits=7)
    low = rest - mid
    return tuple(piece.astype(jnp.bfloat16) for piece in (hi, mid, low))


def selection(offsets, my_index, groups, inner):
    per_row = inner // STRIDE
    off = offsets.reshape(groups, OUTER, per_row)
    rows = jnp.arange(per_row, dtype=jnp.int32)[None, None, :] * STRIDE + off
    rows = rows.transpose(1, 0, 2)
    lanes = jnp.arange(inner, dtype=jnp.int32)
    parity = lax.population_count(rows[:, None, :, :] & lanes[None, :, None, None]) & 1
    group_parity = lax.population_count(jnp.arange(groups, dtype=jnp.int32) & my_index) & 1
    parity = parity ^ group_parity[None, None, :, None]
    return (1 - 2 * parity).astype(jnp.bfloat16).reshape(OUTER, inner, groups * per_row)


def per_device(panel, signs, offsets):
    columns, length = panel.shape
    groups = lax.axis_size("ev")
    levels = groups.bit_length() - 1
    my_index = lax.axis_index("ev")
    inner = length // OUTER
    per_row = inner // STRIDE
    high = lax.Precision.HIGHEST

    signed = panel * signs.astype(jnp.bfloat16)[None, :]
    blocks = signed.reshape(columns, OUTER, inner)
    first = jnp.einsum(
        "xa,cab->xcb",
        hadamard(OUTER).astype(jnp.bfloat16),
        blocks,
        preferred_element_type=jnp.float32,
    )
    pick = selection(offsets, my_index, groups, inner)
    sampled = jnp.einsum(
        "xcb,xbj->xcj",
        first,
        pick.astype(jnp.float32),
        precision=lax.Precision.HIGH,
        preferred_element_type=jnp.float32,
    )
    chunks = sampled.reshape(OUTER, columns, groups, per_row).transpose(2, 1, 0, 3)
    chunks = chunks.reshape(groups, columns, OUTER * per_row)
    own = lax.dynamic_index_in_dim(chunks, my_index, axis=0, keepdims=False)
    arrived = []
    for distance in range(1, groups):
        target = my_index ^ distance
        block = lax.dynamic_index_in_dim(chunks, target, axis=0, keepdims=False)
        pairs = [(source, source ^ distance) for source in range(groups)]
        arrived.append(lax.ppermute(block, "ev", pairs))
    chunks = own
    for block in arrived:
        chunks = chunks + block

    total_events = length * groups
    scale = 1.0 / math.sqrt(total_events * (total_events // STRIDE))
    sketch = chunks * scale
    partial_gram = jnp.dot(
        sketch,
        lax.all_gather(sketch, "col", axis=0, tiled=True).T,
        precision=high,
        preferred_element_type=jnp.float32,
    )
    for start in range(0, levels, 2):
        partial_gram = group_sum(partial_gram, list(range(start, min(start + 2, levels))))
    return partial_gram


def solution(mesh):
    return jax.shard_map(
        per_device,
        mesh=mesh,
        in_specs=(P("col", "ev"), P("ev"), P()),
        out_specs=P("col", None),
        check_vma=False,
    )
```

```python
import math

import jax
import jax.numpy as jnp
from jax import lax
from jax.sharding import PartitionSpec as P

STRIDE = 64
OUTER = 64


def hadamard(order):
    index = jnp.arange(order, dtype=jnp.int32)
    both = index[:, None] & index[None, :]
    parity = jnp.zeros((order, order), jnp.int32)
    for level in range(order.bit_length() - 1):
        parity = parity + (both >> level & 1)
    return (1 - 2 * (parity % 2)).astype(jnp.float32)


def exchange(value, axis, bit):
    mask = 1 << bit
    pairs = [(source, source ^ mask) for source in range(lax.axis_size(axis))]
    return lax.ppermute(value, axis, pairs)


def group_sum(value, bits):
    groups = lax.axis_size("ev")
    masks = [0]
    for bit in bits:
        masks = masks + [mask | (1 << bit) for mask in masks]
    values = [value]
    for mask in masks[1:]:
        pairs = [(source, source ^ mask) for source in range(groups)]
        values.append(lax.ppermute(value, "ev", pairs))
    while len(values) > 1:
        values = [values[i] + values[i + 1] for i in range(0, len(values), 2)]
    return values[0]


def split3(value):
    hi = lax.reduce_precision(value, exponent_bits=8, mantissa_bits=7)
    rest = value - hi
    mid = lax.reduce_precision(rest, exponent_bits=8, mantissa_bits=7)
    low = rest - mid
    return tuple(piece.astype(jnp.bfloat16) for piece in (hi, mid, low))


def selection(offsets, my_index, groups, inner):
    per_row = inner // STRIDE
    off = offsets.reshape(groups, OUTER, per_row)
    rows = jnp.arange(per_row, dtype=jnp.int32)[None, None, :] * STRIDE + off
    rows = rows.transpose(1, 0, 2)
    lanes = jnp.arange(inner, dtype=jnp.int32)
    parity = lax.population_count(rows[:, None, :, :] & lanes[None, :, None, None]) & 1
    group_parity = lax.population_count(jnp.arange(groups, dtype=jnp.int32) & my_index) & 1
    parity = parity ^ group_parity[None, None, :, None]
    return (1 - 2 * parity).astype(jnp.bfloat16).reshape(OUTER, inner, groups * per_row)


def per_device(panel, signs, offsets):
    columns, length = panel.shape
    groups = lax.axis_size("ev")
    levels = groups.bit_length() - 1
    my_index = lax.axis_index("ev")
    inner = length // OUTER
    per_row = inner // STRIDE
    high = lax.Precision.HIGHEST

    signed = panel * signs.astype(jnp.bfloat16)[None, :]
    blocks = signed.reshape(columns, OUTER, inner)
    first = jnp.einsum(
        "xa,cab->xcb",
        hadamard(OUTER).astype(jnp.bfloat16),
        blocks,
        preferred_element_type=jnp.float32,
    )
    pick = selection(offsets, my_index, groups, inner)
    sampled = jnp.einsum(
        "xcb,xbj->xcj",
        first,
        pick.astype(jnp.float32),
        precision=lax.Precision.HIGH,
        preferred_element_type=jnp.float32,
    )
    chunks = sampled.reshape(OUTER, columns, groups, per_row).transpose(2, 1, 0, 3)
    chunks = chunks.reshape(groups, columns, OUTER * per_row)
    own = lax.dynamic_index_in_dim(chunks, my_index, axis=0, keepdims=False)
    arrived = []
    for distance in range(1, groups):
        target = my_index ^ distance
        block = lax.dynamic_index_in_dim(chunks, target, axis=0, keepdims=False)
        pairs = [(source, source ^ distance) for source in range(groups)]
        arrived.append(lax.ppermute(block, "ev", pairs))
    chunks = own
    for block in arrived:
        chunks = chunks + block

    total_events = length * groups
    scale = 1.0 / math.sqrt(total_events * (total_events // STRIDE))
    sketch = chunks * scale
    partial_gram = jnp.dot(
        sketch,
        lax.all_gather(sketch, "col", axis=0, tiled=True).T,
        precision=high,
        preferred_element_type=jnp.float32,
    )
    for start in range(0, levels, 3):
        partial_gram = group_sum(partial_gram, list(range(start, min(start + 3, levels))))
    return partial_gram


def solution(mesh):
    return jax.shard_map(
        per_device,
        mesh=mesh,
        in_specs=(P("col", "ev"), P("ev"), P()),
        out_specs=P("col", None),
        check_vma=False,
    )
```

```python
import math

import jax
import jax.numpy as jnp
from jax import lax
from jax.sharding import PartitionSpec as P

STRIDE = 64
OUTER = 64


def hadamard(order):
    index = jnp.arange(order, dtype=jnp.int32)
    both = index[:, None] & index[None, :]
    parity = jnp.zeros((order, order), jnp.int32)
    for level in range(order.bit_length() - 1):
        parity = parity + (both >> level & 1)
    return (1 - 2 * (parity % 2)).astype(jnp.float32)


def exchange(value, axis, bit):
    mask = 1 << bit
    pairs = [(source, source ^ mask) for source in range(lax.axis_size(axis))]
    return lax.ppermute(value, axis, pairs)


def group_sum(value, bits):
    groups = lax.axis_size("ev")
    masks = [0]
    for bit in bits:
        masks = masks + [mask | (1 << bit) for mask in masks]
    values = [value]
    for mask in masks[1:]:
        pairs = [(source, source ^ mask) for source in range(groups)]
        values.append(lax.ppermute(value, "ev", pairs))
    while len(values) > 1:
        values = [values[i] + values[i + 1] for i in range(0, len(values), 2)]
    return values[0]


def split3(value):
    hi = lax.reduce_precision(value, exponent_bits=8, mantissa_bits=7)
    rest = value - hi
    mid = lax.reduce_precision(rest, exponent_bits=8, mantissa_bits=7)
    low = rest - mid
    return tuple(piece.astype(jnp.bfloat16) for piece in (hi, mid, low))


def selection(offsets, my_index, groups, inner):
    per_row = inner // STRIDE
    off = offsets.reshape(groups, OUTER, per_row)
    rows = jnp.arange(per_row, dtype=jnp.int32)[None, None, :] * STRIDE + off
    rows = rows.transpose(1, 0, 2)
    lanes = jnp.arange(inner, dtype=jnp.int32)
    parity = lax.population_count(rows[:, None, :, :] & lanes[None, :, None, None]) & 1
    group_parity = lax.population_count(jnp.arange(groups, dtype=jnp.int32) & my_index) & 1
    parity = parity ^ group_parity[None, None, :, None]
    return (1 - 2 * parity).astype(jnp.bfloat16).reshape(OUTER, inner, groups * per_row)


def per_device(panel, signs, offsets):
    columns, length = panel.shape
    groups = lax.axis_size("ev")
    levels = groups.bit_length() - 1
    my_index = lax.axis_index("ev")
    inner = length // OUTER
    per_row = inner // STRIDE
    high = lax.Precision.HIGHEST

    signed = panel * signs.astype(jnp.bfloat16)[None, :]
    blocks = signed.reshape(columns, OUTER, inner)
    first = jnp.einsum(
        "xa,cab->xcb",
        hadamard(OUTER).astype(jnp.bfloat16),
        blocks,
        preferred_element_type=jnp.float32,
    )
    pick = lax.optimization_barrier(selection(offsets, my_index, groups, inner).astype(jnp.float32))
    sampled = jnp.einsum(
        "xcb,xbj->xcj",
        first,
        pick,
        precision=lax.Precision.HIGH,
        preferred_element_type=jnp.float32,
    )
    chunks = sampled.reshape(OUTER, columns, groups, per_row).transpose(2, 1, 0, 3)
    chunks = chunks.reshape(groups, columns, OUTER * per_row)
    own = lax.dynamic_index_in_dim(chunks, my_index, axis=0, keepdims=False)
    arrived = []
    for distance in range(1, groups):
        target = my_index ^ distance
        block = lax.dynamic_index_in_dim(chunks, target, axis=0, keepdims=False)
        pairs = [(source, source ^ distance) for source in range(groups)]
        arrived.append(lax.ppermute(block, "ev", pairs))
    chunks = own
    for block in arrived:
        chunks = chunks + block

    total_events = length * groups
    scale = 1.0 / math.sqrt(total_events * (total_events // STRIDE))
    sketch = chunks * scale
    partial_gram = jnp.dot(
        sketch,
        lax.all_gather(sketch, "col", axis=0, tiled=True).T,
        precision=high,
        preferred_element_type=jnp.float32,
    )
    for start in range(0, levels, 2):
        partial_gram = group_sum(partial_gram, list(range(start, min(start + 2, levels))))
    return partial_gram


def solution(mesh):
    return jax.shard_map(
        per_device,
        mesh=mesh,
        in_specs=(P("col", "ev"), P("ev"), P()),
        out_specs=P("col", None),
        check_vma=False,
    )
```

```python
import math

import jax
import jax.numpy as jnp
from jax import lax
from jax.sharding import PartitionSpec as P

STRIDE = 64
OUTER = 32


def hadamard(order):
    index = jnp.arange(order, dtype=jnp.int32)
    both = index[:, None] & index[None, :]
    parity = jnp.zeros((order, order), jnp.int32)
    for level in range(order.bit_length() - 1):
        parity = parity + (both >> level & 1)
    return (1 - 2 * (parity % 2)).astype(jnp.float32)


def exchange(value, axis, bit):
    mask = 1 << bit
    pairs = [(source, source ^ mask) for source in range(lax.axis_size(axis))]
    return lax.ppermute(value, axis, pairs)


def group_sum(value, bits):
    groups = lax.axis_size("ev")
    masks = [0]
    for bit in bits:
        masks = masks + [mask | (1 << bit) for mask in masks]
    values = [value]
    for mask in masks[1:]:
        pairs = [(source, source ^ mask) for source in range(groups)]
        values.append(lax.ppermute(value, "ev", pairs))
    while len(values) > 1:
        values = [values[i] + values[i + 1] for i in range(0, len(values), 2)]
    return values[0]


def split3(value):
    hi = lax.reduce_precision(value, exponent_bits=8, mantissa_bits=7)
    rest = value - hi
    mid = lax.reduce_precision(rest, exponent_bits=8, mantissa_bits=7)
    low = rest - mid
    return tuple(piece.astype(jnp.bfloat16) for piece in (hi, mid, low))


def selection(offsets, my_index, groups, inner):
    per_row = inner // STRIDE
    off = offsets.reshape(groups, OUTER, per_row)
    rows = jnp.arange(per_row, dtype=jnp.int32)[None, None, :] * STRIDE + off
    rows = rows.transpose(1, 0, 2)
    lanes = jnp.arange(inner, dtype=jnp.int32)
    parity = lax.population_count(rows[:, None, :, :] & lanes[None, :, None, None]) & 1
    group_parity = lax.population_count(jnp.arange(groups, dtype=jnp.int32) & my_index) & 1
    parity = parity ^ group_parity[None, None, :, None]
    return (1 - 2 * parity).astype(jnp.bfloat16).reshape(OUTER, inner, groups * per_row)


def per_device(panel, signs, offsets):
    columns, length = panel.shape
    groups = lax.axis_size("ev")
    levels = groups.bit_length() - 1
    my_index = lax.axis_index("ev")
    inner = length // OUTER
    per_row = inner // STRIDE
    high = lax.Precision.HIGHEST

    signed = panel * signs.astype(jnp.bfloat16)[None, :]
    blocks = signed.reshape(columns, OUTER, inner)
    first = jnp.einsum(
        "xa,cab->xcb",
        hadamard(OUTER).astype(jnp.bfloat16),
        blocks,
        preferred_element_type=jnp.float32,
    )
    pick = lax.optimization_barrier(selection(offsets, my_index, groups, inner).astype(jnp.float32))
    sampled = jnp.einsum(
        "xcb,xbj->xcj",
        first,
        pick,
        precision=lax.Precision.HIGH,
        preferred_element_type=jnp.float32,
    )
    chunks = sampled.reshape(OUTER, columns, groups, per_row).transpose(2, 1, 0, 3)
    chunks = chunks.reshape(groups, columns, OUTER * per_row)
    own = lax.dynamic_index_in_dim(chunks, my_index, axis=0, keepdims=False)
    arrived = []
    for distance in range(1, groups):
        target = my_index ^ distance
        block = lax.dynamic_index_in_dim(chunks, target, axis=0, keepdims=False)
        pairs = [(source, source ^ distance) for source in range(groups)]
        arrived.append(lax.ppermute(block, "ev", pairs))
    chunks = own
    for block in arrived:
        chunks = chunks + block

    total_events = length * groups
    scale = 1.0 / math.sqrt(total_events * (total_events // STRIDE))
    sketch = chunks * scale
    partial_gram = jnp.dot(
        sketch,
        lax.all_gather(sketch, "col", axis=0, tiled=True).T,
        precision=high,
        preferred_element_type=jnp.float32,
    )
    for start in range(0, levels, 2):
        partial_gram = group_sum(partial_gram, list(range(start, min(start + 2, levels))))
    return partial_gram


def solution(mesh):
    return jax.shard_map(
        per_device,
        mesh=mesh,
        in_specs=(P("col", "ev"), P("ev"), P()),
        out_specs=P("col", None),
        check_vma=False,
    )
```

```python
import math

import jax
import jax.numpy as jnp
from jax import lax
from jax.sharding import PartitionSpec as P

STRIDE = 64
OUTER = 128


def hadamard(order):
    index = jnp.arange(order, dtype=jnp.int32)
    both = index[:, None] & index[None, :]
    parity = jnp.zeros((order, order), jnp.int32)
    for level in range(order.bit_length() - 1):
        parity = parity + (both >> level & 1)
    return (1 - 2 * (parity % 2)).astype(jnp.float32)


def exchange(value, axis, bit):
    mask = 1 << bit
    pairs = [(source, source ^ mask) for source in range(lax.axis_size(axis))]
    return lax.ppermute(value, axis, pairs)


def group_sum(value, bits):
    groups = lax.axis_size("ev")
    masks = [0]
    for bit in bits:
        masks = masks + [mask | (1 << bit) for mask in masks]
    values = [value]
    for mask in masks[1:]:
        pairs = [(source, source ^ mask) for source in range(groups)]
        values.append(lax.ppermute(value, "ev", pairs))
    while len(values) > 1:
        values = [values[i] + values[i + 1] for i in range(0, len(values), 2)]
    return values[0]


def split3(value):
    hi = lax.reduce_precision(value, exponent_bits=8, mantissa_bits=7)
    rest = value - hi
    mid = lax.reduce_precision(rest, exponent_bits=8, mantissa_bits=7)
    low = rest - mid
    return tuple(piece.astype(jnp.bfloat16) for piece in (hi, mid, low))


def selection(offsets, my_index, groups, inner):
    per_row = inner // STRIDE
    off = offsets.reshape(groups, OUTER, per_row)
    rows = jnp.arange(per_row, dtype=jnp.int32)[None, None, :] * STRIDE + off
    rows = rows.transpose(1, 0, 2)
    lanes = jnp.arange(inner, dtype=jnp.int32)
    parity = lax.population_count(rows[:, None, :, :] & lanes[None, :, None, None]) & 1
    group_parity = lax.population_count(jnp.arange(groups, dtype=jnp.int32) & my_index) & 1
    parity = parity ^ group_parity[None, None, :, None]
    return (1 - 2 * parity).astype(jnp.bfloat16).reshape(OUTER, inner, groups * per_row)


def per_device(panel, signs, offsets):
    columns, length = panel.shape
    groups = lax.axis_size("ev")
    levels = groups.bit_length() - 1
    my_index = lax.axis_index("ev")
    inner = length // OUTER
    per_row = inner // STRIDE
    high = lax.Precision.HIGHEST

    signed = panel * signs.astype(jnp.bfloat16)[None, :]
    blocks = signed.reshape(columns, OUTER, inner)
    first = jnp.einsum(
        "xa,cab->xcb",
        hadamard(OUTER).astype(jnp.bfloat16),
        blocks,
        preferred_element_type=jnp.float32,
    )
    pick = lax.optimization_barrier(selection(offsets, my_index, groups, inner).astype(jnp.float32))
    sampled = jnp.einsum(
        "xcb,xbj->xcj",
        first,
        pick,
        precision=lax.Precision.HIGH,
        preferred_element_type=jnp.float32,
    )
    chunks = sampled.reshape(OUTER, columns, groups, per_row).transpose(2, 1, 0, 3)
    chunks = chunks.reshape(groups, columns, OUTER * per_row)
    own = lax.dynamic_index_in_dim(chunks, my_index, axis=0, keepdims=False)
    arrived = []
    for distance in range(1, groups):
        target = my_index ^ distance
        block = lax.dynamic_index_in_dim(chunks, target, axis=0, keepdims=False)
        pairs = [(source, source ^ distance) for source in range(groups)]
        arrived.append(lax.ppermute(block, "ev", pairs))
    chunks = own
    for block in arrived:
        chunks = chunks + block

    total_events = length * groups
    scale = 1.0 / math.sqrt(total_events * (total_events // STRIDE))
    sketch = chunks * scale
    partial_gram = jnp.dot(
        sketch,
        lax.all_gather(sketch, "col", axis=0, tiled=True).T,
        precision=high,
        preferred_element_type=jnp.float32,
    )
    for start in range(0, levels, 2):
        partial_gram = group_sum(partial_gram, list(range(start, min(start + 2, levels))))
    return partial_gram


def solution(mesh):
    return jax.shard_map(
        per_device,
        mesh=mesh,
        in_specs=(P("col", "ev"), P("ev"), P()),
        out_specs=P("col", None),
        check_vma=False,
    )
```

```python
import math

import jax
import jax.numpy as jnp
from jax import lax
from jax.sharding import PartitionSpec as P

STRIDE = 64
OUTER = 64


def hadamard(order):
    index = jnp.arange(order, dtype=jnp.int32)
    both = index[:, None] & index[None, :]
    parity = jnp.zeros((order, order), jnp.int32)
    for level in range(order.bit_length() - 1):
        parity = parity + (both >> level & 1)
    return (1 - 2 * (parity % 2)).astype(jnp.float32)


def exchange(value, axis, bit):
    mask = 1 << bit
    pairs = [(source, source ^ mask) for source in range(lax.axis_size(axis))]
    return lax.ppermute(value, axis, pairs)


def group_sum(value, bits):
    groups = lax.axis_size("ev")
    masks = [0]
    for bit in bits:
        masks = masks + [mask | (1 << bit) for mask in masks]
    values = [value]
    for mask in masks[1:]:
        pairs = [(source, source ^ mask) for source in range(groups)]
        values.append(lax.ppermute(value, "ev", pairs))
    while len(values) > 1:
        values = [values[i] + values[i + 1] for i in range(0, len(values), 2)]
    return values[0]


def split3(value):
    hi = lax.reduce_precision(value, exponent_bits=8, mantissa_bits=7)
    rest = value - hi
    mid = lax.reduce_precision(rest, exponent_bits=8, mantissa_bits=7)
    low = rest - mid
    return tuple(piece.astype(jnp.bfloat16) for piece in (hi, mid, low))


def selection(offsets, my_index, groups, inner):
    per_row = inner // STRIDE
    off = offsets.reshape(groups, OUTER, per_row)
    rows = jnp.arange(per_row, dtype=jnp.int32)[None, None, :] * STRIDE + off
    rows = rows.transpose(1, 0, 2)
    lanes = jnp.arange(inner, dtype=jnp.int32)
    parity = lax.population_count(rows[:, None, :, :] & lanes[None, :, None, None]) & 1
    group_parity = lax.population_count(jnp.arange(groups, dtype=jnp.int32) & my_index) & 1
    parity = parity ^ group_parity[None, None, :, None]
    return (1 - 2 * parity).astype(jnp.bfloat16).reshape(OUTER, inner, groups * per_row)


def per_device(panel, signs, offsets):
    columns, length = panel.shape
    groups = lax.axis_size("ev")
    levels = groups.bit_length() - 1
    my_index = lax.axis_index("ev")
    inner = length // OUTER
    per_row = inner // STRIDE
    high = lax.Precision.HIGHEST

    signed = panel * signs.astype(jnp.bfloat16)[None, :]
    blocks = signed.reshape(columns, OUTER, inner)
    first = jnp.einsum(
        "xa,cab->xcb",
        hadamard(OUTER).astype(jnp.bfloat16),
        blocks,
        preferred_element_type=jnp.float32,
    )
    pick = lax.optimization_barrier(selection(offsets, my_index, groups, inner))
    sampled = jnp.einsum(
        "xcb,xbj->xcj",
        first,
        pick.astype(jnp.float32),
        precision=lax.Precision.HIGH,
        preferred_element_type=jnp.float32,
    )
    chunks = sampled.reshape(OUTER, columns, groups, per_row).transpose(2, 1, 0, 3)
    chunks = chunks.reshape(groups, columns, OUTER * per_row)
    own = lax.dynamic_index_in_dim(chunks, my_index, axis=0, keepdims=False)
    arrived = []
    for distance in range(1, groups):
        target = my_index ^ distance
        block = lax.dynamic_index_in_dim(chunks, target, axis=0, keepdims=False)
        pairs = [(source, source ^ distance) for source in range(groups)]
        arrived.append(lax.ppermute(block, "ev", pairs))
    chunks = own
    for block in arrived:
        chunks = chunks + block

    total_events = length * groups
    scale = 1.0 / math.sqrt(total_events * (total_events // STRIDE))
    sketch = chunks * scale
    partial_gram = jnp.dot(
        sketch,
        lax.all_gather(sketch, "col", axis=0, tiled=True).T,
        precision=high,
        preferred_element_type=jnp.float32,
    )
    for start in range(0, levels, 2):
        partial_gram = group_sum(partial_gram, list(range(start, min(start + 2, levels))))
    return partial_gram


def solution(mesh):
    return jax.shard_map(
        per_device,
        mesh=mesh,
        in_specs=(P("col", "ev"), P("ev"), P()),
        out_specs=P("col", None),
        check_vma=False,
    )
```

```python
import math

import jax
import jax.numpy as jnp
from jax import lax
from jax.sharding import PartitionSpec as P

STRIDE = 64
OUTER = 64


def hadamard(order):
    index = jnp.arange(order, dtype=jnp.int32)
    both = index[:, None] & index[None, :]
    parity = jnp.zeros((order, order), jnp.int32)
    for level in range(order.bit_length() - 1):
        parity = parity + (both >> level & 1)
    return (1 - 2 * (parity % 2)).astype(jnp.float32)


def exchange(value, axis, bit):
    mask = 1 << bit
    pairs = [(source, source ^ mask) for source in range(lax.axis_size(axis))]
    return lax.ppermute(value, axis, pairs)


def group_sum(value, bits):
    groups = lax.axis_size("ev")
    masks = [0]
    for bit in bits:
        masks = masks + [mask | (1 << bit) for mask in masks]
    values = [value]
    for mask in masks[1:]:
        pairs = [(source, source ^ mask) for source in range(groups)]
        values.append(lax.ppermute(value, "ev", pairs))
    while len(values) > 1:
        values = [values[i] + values[i + 1] for i in range(0, len(values), 2)]
    return values[0]


def selection(offsets, my_index, groups, inner):
    per_row = inner // STRIDE
    off = offsets.reshape(groups, OUTER, per_row)
    rows = jnp.arange(per_row, dtype=jnp.int32)[None, None, :] * STRIDE + off
    rows = rows.transpose(1, 0, 2)
    lanes = jnp.arange(inner, dtype=jnp.int32)
    parity = lax.population_count(rows[:, None, :, :] & lanes[None, :, None, None]) & 1
    group_parity = lax.population_count(jnp.arange(groups, dtype=jnp.int32) & my_index) & 1
    parity = parity ^ group_parity[None, None, :, None]
    return (1 - 2 * parity).astype(jnp.bfloat16).reshape(OUTER, inner, groups * per_row)


def per_device(panel, signs, offsets):
    columns, length = panel.shape
    groups = lax.axis_size("ev")
    levels = groups.bit_length() - 1
    my_index = lax.axis_index("ev")
    inner = length // OUTER
    per_row = inner // STRIDE
    high = lax.Precision.HIGHEST

    signed = panel * signs.astype(jnp.bfloat16)[None, :]
    blocks = signed.reshape(columns, OUTER, inner)
    first = jnp.einsum(
        "xa,cab->xcb",
        hadamard(OUTER).astype(jnp.bfloat16),
        blocks,
        preferred_element_type=jnp.float32,
    )
    pick = lax.optimization_barrier(selection(offsets, my_index, groups, inner))
    high_part = lax.reduce_precision(first, exponent_bits=8, mantissa_bits=7)
    sampled = jnp.einsum(
        "xcb,xbj->xcj", high_part.astype(jnp.bfloat16), pick, preferred_element_type=jnp.float32
    ) + jnp.einsum(
        "xcb,xbj->xcj", (first - high_part).astype(jnp.bfloat16), pick, preferred_element_type=jnp.float32
    )
    chunks = sampled.reshape(OUTER, columns, groups, per_row).transpose(2, 1, 0, 3)
    chunks = chunks.reshape(groups, columns, OUTER * per_row)
    own = lax.dynamic_index_in_dim(chunks, my_index, axis=0, keepdims=False)
    arrived = []
    for distance in range(1, groups):
        target = my_index ^ distance
        block = lax.dynamic_index_in_dim(chunks, target, axis=0, keepdims=False)
        pairs = [(source, source ^ distance) for source in range(groups)]
        arrived.append(lax.ppermute(block, "ev", pairs))
    chunks = own
    for block in arrived:
        chunks = chunks + block

    total_events = length * groups
    scale = 1.0 / math.sqrt(total_events * (total_events // STRIDE))
    sketch = chunks * scale
    partial_gram = jnp.dot(
        sketch,
        lax.all_gather(sketch, "col", axis=0, tiled=True).T,
        precision=high,
        preferred_element_type=jnp.float32,
    )
    for start in range(0, levels, 2):
        partial_gram = group_sum(partial_gram, list(range(start, min(start + 2, levels))))
    return partial_gram


def solution(mesh):
    return jax.shard_map(
        per_device,
        mesh=mesh,
        in_specs=(P("col", "ev"), P("ev"), P()),
        out_specs=P("col", None),
        check_vma=False,
    )
```
